128 devices in a mesh: req: 4 (over y), exp: 32 (over x, z, core).
Axes of the slice: x: 4, y: 4, z: 4, core: 2. Of those that a mesh axis runs over, the one named last changes fastest.
Arguments:
- hidden_in: bfloat16 [16384, 1536], P(('req', 'exp')), may hold values from -6 to 6
- attn_gain: bfloat16 [1536], replicated, may hold values from 0.099609375 to 1.8984375
- w_query: bfloat16 [1536, 1536], replicated, may hold values from -0.625 to 0.625
- w_key: bfloat16 [1536, 512], replicated, may hold values from -0.625 to 0.625
- w_value: bfloat16 [1536, 512], replicated, may hold values from -0.15625 to 0.15625
- w_out: bfloat16 [1536, 1536], replicated, may hold values from -0.15625 to 0.15625
- cache_kv: bfloat16 [4, 1536, 1024], P('req', 'exp'), may hold values from -128 to 128
- cache_len: int32 [4], P('req'), may hold values from 48 to 1536, as said below
- moe_gain: bfloat16 [1536], replicated, may hold values from 0.099609375 to 1.8984375
- expert_ids: int32 [16384, 8], P(('req', 'exp')), may hold values from 0 to 39, all different within a row; in each aligned block of 128 rows (0 to 127, 128 to 255, ...) at most 26 rows name the same one
- expert_weights: bfloat16 [16384, 8], P(('req', 'exp')), may hold values from 0.019897461 to 0.5
- w_gate_up: bfloat16 [32, 5, 1536, 256], P('exp', None, 'req'), may hold values from -0.15625 to 0.15625
- w_down: bfloat16 [32, 5, 128, 1536], P('exp', None, None, 'req'), may hold values from -0.25 to 0.25
Outputs:
- attended: bfloat16 [16384, 1536], P(('req', 'exp'))
- layer_out: bfloat16 [16384, 1536], P(('req', 'exp'))
The draws below stay inside these ranges and needn't reach their ends.
Inputs may be any that keep to these rules, and one draw needn't show every extreme that they name: `cache_len`: cached positions of each request; some request has exactly 1536, some exactly 48. `expert_ids`: each row names 8 different experts. Among the rows of one device no expert is named more than 26 times; in some devices' rows one expert is named exactly 26 times.
All inputs are finite; a program needn't handle non-finite values.
Results may differ from the reference program's by a relative error of at most 0.009.
Values may be sent and summed in bfloat16 or wider, within the bound.
No kernel may reach another device: no remote copies, remote signals or barrier semaphores. Data moves between devices by JAX's collectives and lax.ppermute only.
A program may use at most 256 MiB of HBM per device.

```python
import math
import jax
import jax.numpy as jnp
import numpy as np
from jax import lax

D = 1536
HEADS = 24
KV_HEADS = 8
HEAD_DIM = 64
EXPERTS = 40
FF = 512
TOPK = 8
PIECES = 4
SLICE = 128
GROUP_EXPERTS = 5
TOK_DEV = 128
MOST = 26
NEW = 4096
CACHE = 1536
REQS = 4
TOKENS = 16384
N_EXP = 32


def draw_cache_kv(key, part):
    kv_width = KV_HEADS * HEAD_DIM
    key_main = jax.random.fold_in(key, 0)
    column_scale = jnp.concatenate([jnp.full((kv_width,), 4.0, jnp.float32), jnp.ones((kv_width,), jnp.float32)])
    draws = jnp.clip(jax.random.normal(key_main, (REQS, CACHE, 2 * kv_width), jnp.float32), -4.0, 4.0)
    values = draws * column_scale[None, None, :]
    return values.astype(jnp.bfloat16)


def draw_cache_len(key, part):
    key_len, key_order = jax.random.split(key)
    shortest = max(CACHE // 32, 2)
    lengths = jax.random.randint(key_len, (REQS,), shortest, CACHE + 1, jnp.int32)
    ranking = jax.random.permutation(key_order, REQS)
    return lengths.at[ranking[0]].set(CACHE).at[ranking[1]].set(shortest)


def steps_of(key, dims, shards, smallest, high):
    def one(dim, shards_of):
        steps = jax.random.uniform(jax.random.fold_in(jax.random.fold_in(key, 6), dim), (shards_of,), jnp.float32, smallest / len(shards), high / len(shards))
        return jnp.repeat(jnp.exp(steps), dims[dim] // shards_of).reshape((-1,) + (1,) * (len(dims) - dim - 1))

    level = one(*shards[0])
    for cut in shards[1:]:
        level = level * one(*cut)
    return level


def routed_block(rng, own, number, rows, count, top, limit, skew):
    sequence = jax.random.permutation(rng, count)
    packed, common = portions_of(count, rows * top, limit, skew, True), portions_of(count, rows * top, limit, skew, False)
    places = jnp.arange(count)

    def named(sizes, rotation):
        used = int((sizes > 0).sum())
        fixed = max(1, used // 4)
        moved = fixed + (places - fixed + rotation * (used - fixed)) % max(1, count - fixed)
        return jnp.zeros((count,), jnp.int32).at[sequence[jnp.where(places < fixed, places, moved)]].set(jnp.asarray(sizes, jnp.int32))

    sizes = jnp.where(number % 4 == 0, named(packed, number // 4), named(common, number - number // 4 - 1))
    mixed = jax.random.permutation(jax.random.fold_in(own, 3), count)
    giver, receiver = mixed[0:count // 2 * 2:2], mixed[1:count // 2 * 2:2]
    slack = jnp.minimum(sizes[giver] - 1, limit - sizes[receiver]) // 2
    slack = jnp.where((giver == sequence[0]) | (receiver == sequence[0]) | (sizes[receiver] == 0), 0, jnp.maximum(slack, 0))
    moved = jax.random.randint(jax.random.fold_in(own, 4), (count // 2,), 0, 1 << 20) % (slack + 1)
    sizes = sizes.at[giver].add(-moved).at[receiver].add(moved)
    members = jnp.searchsorted(jnp.cumsum(sizes), jnp.arange(rows * top), side="right").astype(jnp.int32)
    listing = members.reshape(top, rows).T
    listing = listing[jax.random.permutation(jax.random.fold_in(own, 1), rows)]
    rotation = jax.random.randint(jax.random.fold_in(own, 2), (rows, 1), 0, top)
    return jnp.take_along_axis(listing, (jnp.arange(top)[None, :] + rotation) % top, axis=1)


def portions_of(amount, total, bound, slope, full):
    portions = [(1 << 20) // math.isqrt(rank ** slope) + 1 for rank in range(1, amount + 1)]
    largest = bound if full else min(bound, max(-(-total // amount), total * portions[0] // sum(portions)))
    least = 1 if total - largest >= amount - 1 else 0
    holding, rest = [largest] + [least] * (amount - 1), total - largest - least * (amount - 1)
    while rest > 0:
        movable = [i for i in range(1, amount) if holding[i] < largest] or [i for i in range(1, amount) if holding[i] < bound]
        whole, budget = sum([portions[i] for i in movable]), rest
        for i in movable:
            extra = min(bound - holding[i], max(1, budget * portions[i] // whole), rest)
            holding[i] = holding[i] + extra
            rest = rest - extra
    return np.array(holding)


def gaussian(rng, shape, deviation, limit, shards=(), held_as=jnp.bfloat16):
    result = deviation * jax.random.normal(rng, shape, jnp.float32)
    if shards:
        result = result * steps_of(rng, shape, shards, -0.22, 0.18)
    return jnp.clip(result, -limit, limit).astype(held_as)


def setup_inputs(seed: int = 0) -> dict:
    key_of = jax.random.split(jax.random.key(seed), 14)
    hidden_in = gaussian(key_of[0], (TOKENS, D), 1.0, 6.0, ((0, 128),))
    attn_gain = jnp.clip(1.0 + 0.18 * jax.random.normal(key_of[1], (D,), jnp.float32), 0.099609375, 1.8984375).astype(jnp.bfloat16)
    w_query = gaussian(key_of[2], (D, HEADS * HEAD_DIM), (D // 16) ** -0.5, 0.625)
    w_key = gaussian(key_of[3], (D, KV_HEADS * HEAD_DIM), (D // 16) ** -0.5, 0.625)
    w_value = gaussian(key_of[4], (D, KV_HEADS * HEAD_DIM), D ** -0.5, 0.15625)
    w_out = gaussian(key_of[5], (HEADS * HEAD_DIM, D), (HEADS * HEAD_DIM) ** -0.5, 0.15625)
    cache_kv = draw_cache_kv(jax.random.fold_in(key_of[13], 71), 0)
    cache_len = draw_cache_len(jax.random.fold_in(key_of[13], 71), 0)
    moe_gain = jnp.clip(1.0 + 0.18 * jax.random.normal(key_of[8], (D,), jnp.float32), 0.099609375, 1.8984375).astype(jnp.bfloat16)
    expert_ids_keys = jax.random.split(jax.random.fold_in(key_of[9], 1), TOKENS // TOK_DEV)
    expert_ids_turns = jax.random.permutation(jax.random.fold_in(key_of[9], 3), TOKENS // TOK_DEV)
    expert_ids = jax.vmap(lambda own, number: routed_block(jax.random.fold_in(key_of[9], 2), own, number, TOK_DEV, EXPERTS, TOPK, MOST, 1))(expert_ids_keys, expert_ids_turns).reshape((TOKENS, TOPK))
    expert_weights = jnp.clip(jnp.exp(math.log(0.5) - 3.224016 * jax.random.uniform(key_of[10], (TOKENS, TOPK), jnp.float32) ** steps_of(key_of[10], (TOKENS, TOPK), ((0, 128),), -0.2, 0.2)), 0.019897461, 0.5).astype(jnp.bfloat16)
    w_gate_up = gaussian(key_of[11], (N_EXP, GROUP_EXPERTS, D, 2 * SLICE), D ** -0.5, 0.15625, ((0, 32), (2, 4)))
    w_down = gaussian(key_of[12], (N_EXP, GROUP_EXPERTS, SLICE, D), FF ** -0.5, 0.25, ((0, 32), (3, 4)))
    return {"hidden_in": hidden_in, "attn_gain": attn_gain, "w_query": w_query, "w_key": w_key, "w_value": w_value, "w_out": w_out, "cache_kv": cache_kv, "cache_len": cache_len, "moe_gain": moe_gain, "expert_ids": expert_ids, "expert_weights": expert_weights, "w_gate_up": w_gate_up, "w_down": w_down}


rope_base = 10000.0
attn_scale = 0.015625
residual_scale = 1.0
norm_eps = 1e-06
neg_fill = -1e+30

def rms_scale(values, gain):
    widened = values.astype(jnp.float32)
    mean_sq = lax.optimization_barrier(jnp.mean(widened * widened, axis=-1, keepdims=True))
    return (widened * lax.rsqrt(mean_sq + norm_eps) * gain.astype(jnp.float32)).astype(jnp.bfloat16)

def rotate(projected, positions, head_count, head_dim):
    row_count = projected.shape[0]
    shaped = projected.reshape(row_count, head_count, head_dim)
    half_dim = head_dim // 2
    inverse_freq = rope_base ** (-(jnp.arange(half_dim, dtype=jnp.float32) * 2.0 / head_dim))
    angles = positions.astype(jnp.float32)[:, None] * inverse_freq[None, :]
    cosine = jnp.cos(angles)[:, None, :]
    sinus = jnp.sin(angles)[:, None, :]
    lower_half = shaped[..., :half_dim]
    upper_half = shaped[..., half_dim:]
    turned = jnp.concatenate([lower_half * cosine - upper_half * sinus, upper_half * cosine + lower_half * sinus], axis=-1)
    return turned.reshape(row_count, head_count * head_dim).astype(jnp.bfloat16)

def attend_request(query, key_rows, value_rows, length):
    new_total = query.shape[0]
    group_size = HEADS // KV_HEADS
    key_count = key_rows.shape[0]
    key_heads = key_rows.astype(jnp.float32).reshape(key_count, KV_HEADS, HEAD_DIM)
    value_heads = value_rows.astype(jnp.float32).reshape(key_count, KV_HEADS, HEAD_DIM)
    key_index = jnp.arange(key_count, dtype=jnp.int32)
    block_rows = min(512, new_total)

    def one_block(first_row):
        query_block = lax.dynamic_slice_in_dim(query, first_row, block_rows, 0).astype(jnp.float32)
        query_block = query_block.reshape(block_rows, KV_HEADS, group_size, HEAD_DIM)
        scores = jnp.einsum('tkgd,rkd->tkgr', query_block, key_heads) * attn_scale
        query_index = first_row + jnp.arange(block_rows, dtype=jnp.int32)
        visible = jnp.where(key_index[None, :] < CACHE, (key_index < length)[None, :], (key_index - CACHE)[None, :] <= query_index[:, None])
        scores = jnp.where(visible[:, None, None, :], scores, neg_fill)
        top_score = lax.optimization_barrier(jnp.max(scores, axis=-1, keepdims=True))
        weights = jnp.where(visible[:, None, None, :], jnp.exp(scores - top_score), 0.0)
        total_sum = lax.optimization_barrier(jnp.sum(weights, axis=-1))
        rounded = lax.optimization_barrier(weights.astype(jnp.bfloat16)).astype(jnp.float32)
        context = jnp.einsum('tkgr,rkd->tkgd', rounded, value_heads) / total_sum[..., None]
        return context.reshape(block_rows, HEADS * HEAD_DIM).astype(jnp.bfloat16)
    starts = jnp.arange(new_total // block_rows, dtype=jnp.int32) * block_rows
    return lax.map(one_block, starts).reshape(new_total, HEADS * HEAD_DIM)

def reference(hidden_in, attn_gain, w_query, w_key, w_value, w_out, cache_kv, cache_len, moe_gain, expert_ids, expert_weights, w_gate_up, w_down):
    kv_width = KV_HEADS * HEAD_DIM
    normed = rms_scale(hidden_in, attn_gain)
    token_index = jnp.arange(NEW, dtype=jnp.int32)
    contexts = []
    for request in range(REQS):
        request_rows = normed[request * NEW:(request + 1) * NEW]
        positions = cache_len[request] + token_index
        query = rotate(jnp.dot(request_rows, w_query, preferred_element_type=jnp.float32), positions, HEADS, HEAD_DIM)
        keys_new = rotate(jnp.dot(request_rows, w_key, preferred_element_type=jnp.float32), positions, KV_HEADS, HEAD_DIM)
        values_new = jnp.dot(request_rows, w_value, preferred_element_type=jnp.float32).astype(jnp.bfloat16)
        key_rows = jnp.concatenate([cache_kv[request, :, :kv_width], keys_new], axis=0)
        value_rows = jnp.concatenate([cache_kv[request, :, kv_width:], values_new], axis=0)
        contexts.append(attend_request(query, key_rows, value_rows, cache_len[request]))
    context = jnp.concatenate(contexts, axis=0)
    projected = jnp.dot(context, w_out, preferred_element_type=jnp.float32)
    attended = (hidden_in.astype(jnp.float32) + residual_scale * projected).astype(jnp.bfloat16)
    moe_in = rms_scale(attended, moe_gain)
    blocks = N_EXP // PIECES
    gate_up = w_gate_up.reshape(blocks, PIECES, GROUP_EXPERTS, D, 2 * SLICE).transpose(0, 2, 1, 3, 4).reshape(EXPERTS, PIECES, D, 2 * SLICE)
    down_rows = w_down.reshape(blocks, PIECES, GROUP_EXPERTS, SLICE, D).transpose(0, 2, 1, 3, 4).reshape(EXPERTS, PIECES, SLICE, D)
    flat_ids = expert_ids.reshape(-1)
    flat_weights = expert_weights.reshape(-1).astype(jnp.float32)
    pair_count = flat_ids.shape[0]
    token_of = jnp.arange(pair_count, dtype=jnp.int32) // TOPK
    ranking = jnp.argsort(flat_ids, stable=True).astype(jnp.int32)
    expert_loads = lax.optimization_barrier(jnp.sum((flat_ids[:, None] == jnp.arange(EXPERTS, dtype=jnp.int32)[None, :]).astype(jnp.int32), axis=0))
    offsets = jnp.cumsum(expert_loads) - expert_loads
    capacity = TOKENS // TOK_DEV * MOST
    slot_rank = jnp.arange(capacity, dtype=jnp.int32)
    occupied = slot_rank[None, :] < expert_loads[:, None]
    chosen = ranking[jnp.minimum(offsets[:, None] + slot_rank[None, :], pair_count - 1)]
    tokens_sel = token_of[chosen]
    weight_sel = jnp.where(occupied, flat_weights[chosen], 0.0)

    def expert_step(running, inputs):
        gate_e, down_e, tokens_e, weight_e = inputs
        rows_e = moe_in[tokens_e].astype(jnp.float32)
        gated = jnp.einsum('cd,qdf->qcf', rows_e, gate_e.astype(jnp.float32))
        activ = (jax.nn.silu(gated[..., :SLICE]) * gated[..., SLICE:]).astype(jnp.bfloat16)
        activ = lax.optimization_barrier(activ).astype(jnp.float32)
        partial_value = jnp.einsum('qcf,qfd->qcd', activ, down_e.astype(jnp.float32)).astype(jnp.bfloat16)
        partial_value = lax.optimization_barrier(partial_value).astype(jnp.float32)
        weighted = weight_e[:, None] * lax.optimization_barrier(jnp.sum(partial_value, axis=0))
        return (running.at[tokens_e].add(weighted), None)
    mixture, _ = lax.scan(expert_step, jnp.zeros((TOKENS, D), jnp.float32), (gate_up, down_rows, tokens_sel, weight_sel))
    layer_out = (attended.astype(jnp.float32) + residual_scale * mixture).astype(jnp.bfloat16)
    return (attended, layer_out)
```

```python
import jax
import jax.numpy as jnp
from jax import lax
from jax.sharding import Mesh, PartitionSpec as P

HEAD_DIM = 64
EXPERTS = 40
TOPK = 8
PIECES = 4
MOST = 26


rope_base = 10000.0
attn_scale = 0.015625
residual_scale = 1.0
norm_eps = 1e-06
neg_fill = -1e30
key_block = 512


def rms_scale(values, gain):
    widened = values.astype(jnp.float32)
    mean_sq = jnp.mean(widened * widened, axis=-1, keepdims=True)
    return (widened * lax.rsqrt(mean_sq + norm_eps) * gain.astype(jnp.float32)).astype(jnp.bfloat16)


def rotate(projected, positions, head_count, head_dim):
    row_count = projected.shape[0]
    shaped = projected.reshape(row_count, head_count, head_dim)
    half_dim = head_dim // 2
    inverse_freq = rope_base ** (-(jnp.arange(half_dim, dtype=jnp.float32) * 2.0 / head_dim))
    angles = positions.astype(jnp.float32)[:, None] * inverse_freq[None, :]
    cosine = jnp.cos(angles)[:, None, :]
    sinus = jnp.sin(angles)[:, None, :]
    lower_half = shaped[..., :half_dim]
    upper_half = shaped[..., half_dim:]
    turned = jnp.concatenate(
        [lower_half * cosine - upper_half * sinus, upper_half * cosine + lower_half * sinus],
        axis=-1,
    )
    return turned.reshape(row_count, head_count * head_dim).astype(jnp.bfloat16)


def attend_block(running, queries, block_rows, visible, kv_width):
    run_max, run_sum, run_acc = running
    kv_heads = run_max.shape[0]
    head_dim = run_acc.shape[-1]
    block_size = block_rows.shape[0]
    key_heads = block_rows[:, :kv_width].reshape(block_size, kv_heads, head_dim)
    value_heads = block_rows[:, kv_width:].reshape(block_size, kv_heads, head_dim)
    scores = (
        jnp.einsum("tkgd,rkd->kgtr", queries, key_heads, preferred_element_type=jnp.float32)
        * attn_scale
    )
    scores = jnp.where(visible[None, None], scores, neg_fill)
    new_max = jnp.maximum(run_max, jnp.max(scores, axis=-1))
    weights = jnp.where(visible[None, None], jnp.exp(scores - new_max[..., None]), 0.0)
    factor = jnp.exp(run_max - new_max)
    new_sum = run_sum * factor + jnp.sum(weights, axis=-1)
    new_acc = run_acc * factor[..., None] + jnp.einsum(
        "kgtr,rkd->kgtd",
        weights.astype(jnp.bfloat16),
        value_heads,
        preferred_element_type=jnp.float32,
    )
    return (new_max, new_sum, new_acc)


def shards(
    hidden_in,
    attn_gain,
    w_query,
    w_key,
    w_value,
    w_out,
    cache_kv,
    cache_len,
    moe_gain,
    expert_ids,
    expert_weights,
    w_gate_up,
    w_down,
):
    rows_here = hidden_in.shape[0]
    width = hidden_in.shape[1]
    kv_width = w_key.shape[1]
    kv_heads = kv_width // HEAD_DIM
    head_count = w_query.shape[1] // HEAD_DIM
    group_size = head_count // kv_heads
    position_exp = lax.axis_index("xz") * lax.axis_size("core") + lax.axis_index("core")
    length = cache_len[0]
    cache_rows = cache_kv[0]
    cache_count = cache_rows.shape[0]
    gate_up_full, down_full = (
        lax.all_gather(lax.all_gather(w_gate_up[0], "req", axis=1, tiled=True), "core", axis=0),
        lax.all_gather(lax.all_gather(w_down[0], "req", axis=2, tiled=True), "core", axis=0),
    )
    normed = rms_scale(hidden_in, attn_gain)
    query_pos = position_exp * rows_here + jnp.arange(rows_here, dtype=jnp.int32)
    positions = length + query_pos
    query = rotate(
        jnp.dot(normed, w_query, preferred_element_type=jnp.float32),
        positions,
        head_count,
        HEAD_DIM,
    )
    keys_new = rotate(
        jnp.dot(normed, w_key, preferred_element_type=jnp.float32), positions, kv_heads, HEAD_DIM
    )
    values_new = jnp.dot(normed, w_value, preferred_element_type=jnp.float32).astype(jnp.bfloat16)
    new_kv = jnp.concatenate([keys_new, values_new], axis=1)
    queries = query.reshape(rows_here, kv_heads, group_size, HEAD_DIM)
    initial = (
        jnp.full((kv_heads, group_size, rows_here), neg_fill, jnp.float32),
        jnp.zeros((kv_heads, group_size, rows_here), jnp.float32),
        jnp.zeros((kv_heads, group_size, rows_here, HEAD_DIM), jnp.float32),
    )
    shard_rows = cache_count + rows_here
    joined = jnp.concatenate([cache_rows, new_kv], axis=0)
    running = initial
    piece = lax.all_gather(joined, ("xz", "core"), axis=0, tiled=True)
    first_row = jnp.int32(0)
    key_count = piece.shape[0]
    for offset in range(0, key_count, key_block):
        block_size = min(key_block, key_count - offset)
        key_index = first_row + offset + jnp.arange(block_size, dtype=jnp.int32)
        owner = key_index // shard_rows
        within = key_index - owner * shard_rows
        cached = within < cache_count
        cache_pos = owner * cache_count + within
        new_pos = owner * rows_here + within - cache_count
        running = attend_block(
            running,
            queries,
            piece[offset : offset + block_size],
            jnp.where(
                cached[None, :],
                (cache_pos < length)[None, :],
                new_pos[None, :] <= query_pos[:, None],
            ),
            kv_width,
        )
    run_max, run_sum, run_acc = running
    context = (
        (run_acc / run_sum[..., None])
        .transpose(2, 0, 1, 3)
        .reshape(rows_here, head_count * HEAD_DIM)
        .astype(jnp.bfloat16)
    )
    projected = jnp.dot(context, w_out, preferred_element_type=jnp.float32)
    attended = (hidden_in.astype(jnp.float32) + residual_scale * projected).astype(jnp.bfloat16)
    moe_in = rms_scale(attended, moe_gain)
    block_experts = gate_up_full.shape[1]
    slice_width = down_full.shape[2]
    pairs = lax.axis_size("xz") // (EXPERTS // block_experts)
    flat_ids = expert_ids.reshape(-1)
    matches = (flat_ids[:, None] == jnp.arange(EXPERTS, dtype=jnp.int32)[None, :]).astype(jnp.int32)
    slot_rank = jnp.sum((jnp.cumsum(matches, axis=0) - matches) * matches, axis=1)
    slot_index = flat_ids * MOST + slot_rank
    token_of = jnp.arange(flat_ids.shape[0], dtype=jnp.int32) // TOPK
    sectioned = (
        jnp.zeros((EXPERTS * MOST, width), jnp.bfloat16).at[slot_index].set(moe_in[token_of])
    )
    blocks = EXPERTS // block_experts
    outgoing = jnp.broadcast_to(
        sectioned.reshape(blocks, 1, block_experts, MOST, width),
        (blocks, pairs, block_experts, MOST, width),
    )
    outgoing = outgoing.reshape(blocks * pairs, block_experts, MOST, width)
    gate_up = jnp.einsum(
        "skmd,ckdf->sckmf",
        lax.all_to_all(outgoing, "xz", split_axis=0, concat_axis=0, tiled=True),
        gate_up_full,
        preferred_element_type=jnp.float32,
    )
    activated = (jax.nn.silu(gate_up[..., :slice_width]) * gate_up[..., slice_width:]).astype(
        jnp.bfloat16
    )
    computed = jnp.einsum(
        "sckmf,ckfd->sckmd", activated, down_full, preferred_element_type=jnp.float32
    ).astype(jnp.bfloat16)
    computed = jnp.sum(computed, axis=1, dtype=jnp.float32).astype(jnp.bfloat16)
    returned = lax.all_to_all(computed, "xz", split_axis=0, concat_axis=0, tiled=True)
    summed = jnp.sum(
        returned.reshape(blocks, pairs, block_experts, MOST, width), axis=1, dtype=jnp.float32
    )
    summed = summed.reshape(EXPERTS * MOST, width)
    picked = summed[slot_index] * expert_weights.reshape(-1).astype(jnp.float32)[:, None]
    mixture = jnp.sum(picked.reshape(rows_here, TOPK, width), axis=1)
    layer_out = (attended.astype(jnp.float32) + residual_scale * mixture).astype(jnp.bfloat16)
    return (attended, layer_out)


def solution(mesh):
    req_size, exp_size = mesh.shape["req"], mesh.shape["exp"]
    mesh = Mesh(mesh.devices.reshape(req_size, exp_size // 2, 2), ("req", "xz", "core"))
    rows = ("req", "xz", "core")
    cols = ("xz", "core")
    in_specs = (
        P(rows, None),
        P(),
        P(),
        P(),
        P(),
        P(),
        P("req", cols, None),
        P("req"),
        P(),
        P(rows, None),
        P(rows, None),
        P(cols, None, "req", None),
        P(cols, None, None, "req"),
    )
    out_specs = (P(rows, None), P(rows, None))
    return jax.shard_map(shards, mesh=mesh, in_specs=in_specs, out_specs=out_specs, check_vma=False)
```

```python
import jax
import jax.numpy as jnp
from jax import lax
from jax.sharding import Mesh, PartitionSpec as P

HEAD_DIM = 64
EXPERTS = 40
TOPK = 8
PIECES = 4
MOST = 26


rope_base = 10000.0
attn_scale = 0.015625
residual_scale = 1.0
norm_eps = 1e-06
neg_fill = -1e30
key_block = 512


def rms_scale(values, gain):
    widened = values.astype(jnp.float32)
    mean_sq = jnp.mean(widened * widened, axis=-1, keepdims=True)
    return (widened * lax.rsqrt(mean_sq + norm_eps) * gain.astype(jnp.float32)).astype(jnp.bfloat16)


def rotate(projected, positions, head_count, head_dim):
    row_count = projected.shape[0]
    shaped = projected.reshape(row_count, head_count, head_dim)
    half_dim = head_dim // 2
    inverse_freq = rope_base ** (-(jnp.arange(half_dim, dtype=jnp.float32) * 2.0 / head_dim))
    angles = positions.astype(jnp.float32)[:, None] * inverse_freq[None, :]
    cosine = jnp.cos(angles)[:, None, :]
    sinus = jnp.sin(angles)[:, None, :]
    lower_half = shaped[..., :half_dim]
    upper_half = shaped[..., half_dim:]
    turned = jnp.concatenate(
        [lower_half * cosine - upper_half * sinus, upper_half * cosine + lower_half * sinus],
        axis=-1,
    )
    return turned.reshape(row_count, head_count * head_dim).astype(jnp.bfloat16)


def attend_block(running, queries, block_rows, visible, kv_width):
    run_max, run_sum, run_acc = running
    kv_heads = run_max.shape[0]
    head_dim = run_acc.shape[-1]
    block_size = block_rows.shape[0]
    key_heads = block_rows[:, :kv_width].reshape(block_size, kv_heads, head_dim)
    value_heads = block_rows[:, kv_width:].reshape(block_size, kv_heads, head_dim)
    scores = (
        jnp.einsum("tkgd,rkd->kgtr", queries, key_heads, preferred_element_type=jnp.float32)
        * attn_scale
    )
    scores = jnp.where(visible[None, None], scores, neg_fill)
    new_max = jnp.maximum(run_max, jnp.max(scores, axis=-1))
    weights = jnp.where(visible[None, None], jnp.exp(scores - new_max[..., None]), 0.0)
    factor = jnp.exp(run_max - new_max)
    new_sum = run_sum * factor + jnp.sum(weights, axis=-1)
    new_acc = run_acc * factor[..., None] + jnp.einsum(
        "kgtr,rkd->kgtd",
        weights.astype(jnp.bfloat16),
        value_heads,
        preferred_element_type=jnp.float32,
    )
    return (new_max, new_sum, new_acc)


def shards(
    hidden_in,
    attn_gain,
    w_query,
    w_key,
    w_value,
    w_out,
    cache_kv,
    cache_len,
    moe_gain,
    expert_ids,
    expert_weights,
    w_gate_up,
    w_down,
):
    rows_here = hidden_in.shape[0]
    width = hidden_in.shape[1]
    kv_width = w_key.shape[1]
    kv_heads = kv_width // HEAD_DIM
    head_count = w_query.shape[1] // HEAD_DIM
    group_size = head_count // kv_heads
    position_exp = lax.axis_index("xz") * lax.axis_size("core") + lax.axis_index("core")
    length = cache_len[0]
    cache_rows = cache_kv[0]
    cache_count = cache_rows.shape[0]
    cache_all = lax.all_gather(cache_rows, ("xz", "core"), axis=0, tiled=True)
    normed = rms_scale(hidden_in, attn_gain)
    query_pos = position_exp * rows_here + jnp.arange(rows_here, dtype=jnp.int32)
    positions = length + query_pos
    query = rotate(
        jnp.dot(normed, w_query, preferred_element_type=jnp.float32),
        positions,
        head_count,
        HEAD_DIM,
    )
    keys_new = rotate(
        jnp.dot(normed, w_key, preferred_element_type=jnp.float32), positions, kv_heads, HEAD_DIM
    )
    values_new = jnp.dot(normed, w_value, preferred_element_type=jnp.float32).astype(jnp.bfloat16)
    new_kv = jnp.concatenate([keys_new, values_new], axis=1)
    queries = query.reshape(rows_here, kv_heads, group_size, HEAD_DIM)
    initial = (
        jnp.full((kv_heads, group_size, rows_here), neg_fill, jnp.float32),
        jnp.zeros((kv_heads, group_size, rows_here), jnp.float32),
        jnp.zeros((kv_heads, group_size, rows_here, HEAD_DIM), jnp.float32),
    )
    running = initial
    for offset in range(0, cache_all.shape[0], key_block):
        block_size = min(key_block, cache_all.shape[0] - offset)
        cache_pos = offset + jnp.arange(block_size, dtype=jnp.int32)
        running = attend_block(
            running,
            queries,
            cache_all[offset : offset + block_size],
            jnp.broadcast_to((cache_pos < length)[None, :], (rows_here, block_size)),
            kv_width,
        )
    new_all = lax.all_gather(new_kv, ("xz", "core"), axis=0, tiled=True)
    gate_up_local, down_local, new_all = lax.optimization_barrier((w_gate_up[0], w_down[0], new_all))
    gate_up_full, down_full = (
        lax.all_gather(lax.all_gather(gate_up_local, "req", axis=1, tiled=True), "core", axis=0),
        lax.all_gather(lax.all_gather(down_local, "req", axis=2, tiled=True), "core", axis=0),
    )
    for offset in range(0, new_all.shape[0], key_block):
        block_size = min(key_block, new_all.shape[0] - offset)
        new_pos = offset + jnp.arange(block_size, dtype=jnp.int32)
        running = attend_block(
            running,
            queries,
            new_all[offset : offset + block_size],
            new_pos[None, :] <= query_pos[:, None],
            kv_width,
        )
    run_max, run_sum, run_acc = running
    context = (
        (run_acc / run_sum[..., None])
        .transpose(2, 0, 1, 3)
        .reshape(rows_here, head_count * HEAD_DIM)
        .astype(jnp.bfloat16)
    )
    projected = jnp.dot(context, w_out, preferred_element_type=jnp.float32)
    attended = (hidden_in.astype(jnp.float32) + residual_scale * projected).astype(jnp.bfloat16)
    moe_in = rms_scale(attended, moe_gain)
    block_experts = gate_up_full.shape[1]
    slice_width = down_full.shape[2]
    pairs = lax.axis_size("xz") // (EXPERTS // block_experts)
    flat_ids = expert_ids.reshape(-1)
    matches = (flat_ids[:, None] == jnp.arange(EXPERTS, dtype=jnp.int32)[None, :]).astype(jnp.int32)
    pair_count = flat_ids.shape[0]
    earlier = (
        jnp.arange(pair_count, dtype=jnp.int32)[None, :] < jnp.arange(pair_count, dtype=jnp.int32)[:, None]
    ).astype(jnp.bfloat16)
    before = jnp.dot(earlier, matches.astype(jnp.bfloat16), preferred_element_type=jnp.float32)
    slot_rank = jnp.sum(before.astype(jnp.int32) * matches, axis=1)
    slot_index = flat_ids * MOST + slot_rank
    token_of = jnp.arange(flat_ids.shape[0], dtype=jnp.int32) // TOPK
    slot_token = jnp.zeros((EXPERTS * MOST,), jnp.int32).at[slot_index].set(token_of)
    blocks = EXPERTS // block_experts
    slot_token = jnp.broadcast_to(
        slot_token.reshape(blocks, 1, block_experts, MOST), (blocks, pairs, block_experts, MOST)
    ).reshape(blocks * pairs, block_experts, MOST)
    outgoing = moe_in[slot_token]
    gate_up = jnp.einsum(
        "skmd,ckdf->sckmf",
        lax.all_to_all(outgoing, "xz", split_axis=0, concat_axis=0, tiled=True),
        gate_up_full,
        preferred_element_type=jnp.float32,
    )
    activated = (jax.nn.silu(gate_up[..., :slice_width]) * gate_up[..., slice_width:]).astype(
        jnp.bfloat16
    )
    computed = jnp.einsum(
        "sckmf,ckfd->sckmd", activated, down_full, preferred_element_type=jnp.float32
    ).astype(jnp.bfloat16)
    computed = jnp.sum(computed, axis=1, dtype=jnp.float32).astype(jnp.bfloat16)
    returned = lax.all_to_all(computed, "xz", split_axis=0, concat_axis=0, tiled=True)
    summed = jnp.sum(
        returned.reshape(blocks, pairs, block_experts, MOST, width), axis=1, dtype=jnp.float32
    )
    summed = summed.reshape(EXPERTS * MOST, width)
    picked = summed[slot_index] * expert_weights.reshape(-1).astype(jnp.float32)[:, None]
    mixture = jnp.sum(picked.reshape(rows_here, TOPK, width), axis=1)
    layer_out = (attended.astype(jnp.float32) + residual_scale * mixture).astype(jnp.bfloat16)
    return (attended, layer_out)


def solution(mesh):
    req_size, exp_size = mesh.shape["req"], mesh.shape["exp"]
    mesh = Mesh(mesh.devices.reshape(req_size, exp_size // 2, 2), ("req", "xz", "core"))
    rows = ("req", "xz", "core")
    cols = ("xz", "core")
    in_specs = (
        P(rows, None),
        P(),
        P(),
        P(),
        P(),
        P(),
        P("req", cols, None),
        P("req"),
        P(),
        P(rows, None),
        P(rows, None),
        P(cols, None, "req", None),
        P(cols, None, None, "req"),
    )
    out_specs = (P(rows, None), P(rows, None))
    return jax.shard_map(shards, mesh=mesh, in_specs=in_specs, out_specs=out_specs, check_vma=False)
```

```python
import jax
import jax.numpy as jnp
from jax import lax
from jax.sharding import Mesh, PartitionSpec as P

HEAD_DIM = 64
EXPERTS = 40
TOPK = 8
PIECES = 4
MOST = 26


rope_base = 10000.0
attn_scale = 0.015625
residual_scale = 1.0
norm_eps = 1e-06
neg_fill = -1e30
key_block = 512
EXP_AXES = ("x", "zhi", "zlo", "core")


def rms_scale(values, gain):
    widened = values.astype(jnp.float32)
    mean_sq = jnp.mean(widened * widened, axis=-1, keepdims=True)
    return (widened * lax.rsqrt(mean_sq + norm_eps) * gain.astype(jnp.float32)).astype(jnp.bfloat16)


def rotate(projected, positions, head_count, head_dim):
    row_count = projected.shape[0]
    shaped = projected.reshape(row_count, head_count, head_dim)
    half_dim = head_dim // 2
    inverse_freq = rope_base ** (-(jnp.arange(half_dim, dtype=jnp.float32) * 2.0 / head_dim))
    angles = positions.astype(jnp.float32)[:, None] * inverse_freq[None, :]
    cosine = jnp.cos(angles)[:, None, :]
    sinus = jnp.sin(angles)[:, None, :]
    lower_half = shaped[..., :half_dim]
    upper_half = shaped[..., half_dim:]
    turned = jnp.concatenate(
        [lower_half * cosine - upper_half * sinus, upper_half * cosine + lower_half * sinus],
        axis=-1,
    )
    return turned.reshape(row_count, head_count * head_dim).astype(jnp.bfloat16)


def attend_block(running, queries, block_rows, visible, kv_width):
    run_max, run_sum, run_acc = running
    kv_heads = run_max.shape[0]
    head_dim = run_acc.shape[-1]
    block_size = block_rows.shape[0]
    key_heads = block_rows[:, :kv_width].reshape(block_size, kv_heads, head_dim)
    value_heads = block_rows[:, kv_width:].reshape(block_size, kv_heads, head_dim)
    scores = (
        jnp.einsum("tkgd,rkd->kgtr", queries, key_heads, preferred_element_type=jnp.float32)
        * attn_scale
    )
    scores = jnp.where(visible[None, None], scores, neg_fill)
    new_max = jnp.maximum(run_max, jnp.max(scores, axis=-1))
    weights = jnp.where(visible[None, None], jnp.exp(scores - new_max[..., None]), 0.0)
    factor = jnp.exp(run_max - new_max)
    new_sum = run_sum * factor + jnp.sum(weights, axis=-1)
    new_acc = run_acc * factor[..., None] + jnp.einsum(
        "kgtr,rkd->kgtd",
        weights.astype(jnp.bfloat16),
        value_heads,
        preferred_element_type=jnp.float32,
    )
    return (new_max, new_sum, new_acc)


def shards(
    hidden_in,
    attn_gain,
    w_query,
    w_key,
    w_value,
    w_out,
    cache_kv,
    cache_len,
    moe_gain,
    expert_ids,
    expert_weights,
    w_gate_up,
    w_down,
):
    rows_here = hidden_in.shape[0]
    width = hidden_in.shape[1]
    kv_width = w_key.shape[1]
    kv_heads = kv_width // HEAD_DIM
    head_count = w_query.shape[1] // HEAD_DIM
    group_size = head_count // kv_heads
    core = lax.axis_index("core")
    position_exp = (
        (lax.axis_index("x") * lax.axis_size("zhi") + lax.axis_index("zhi")) * lax.axis_size("zlo")
        + lax.axis_index("zlo")
    ) * lax.axis_size("core") + core
    length = cache_len[0]
    cache_rows = cache_kv[0]
    cache_count = cache_rows.shape[0]
    cache_all = lax.all_gather(cache_rows, EXP_AXES, axis=0, tiled=True)
    normed = rms_scale(hidden_in, attn_gain)
    query_pos = position_exp * rows_here + jnp.arange(rows_here, dtype=jnp.int32)
    positions = length + query_pos
    query = rotate(
        jnp.dot(normed, w_query, preferred_element_type=jnp.float32),
        positions,
        head_count,
        HEAD_DIM,
    )
    keys_new = rotate(
        jnp.dot(normed, w_key, preferred_element_type=jnp.float32), positions, kv_heads, HEAD_DIM
    )
    values_new = jnp.dot(normed, w_value, preferred_element_type=jnp.float32).astype(jnp.bfloat16)
    new_kv = jnp.concatenate([keys_new, values_new], axis=1)
    queries = query.reshape(rows_here, kv_heads, group_size, HEAD_DIM)
    initial = (
        jnp.full((kv_heads, group_size, rows_here), neg_fill, jnp.float32),
        jnp.zeros((kv_heads, group_size, rows_here), jnp.float32),
        jnp.zeros((kv_heads, group_size, rows_here, HEAD_DIM), jnp.float32),
    )
    running = initial
    for offset in range(0, cache_all.shape[0], key_block):
        block_size = min(key_block, cache_all.shape[0] - offset)
        cache_pos = offset + jnp.arange(block_size, dtype=jnp.int32)
        running = attend_block(
            running,
            queries,
            cache_all[offset : offset + block_size],
            jnp.broadcast_to((cache_pos < length)[None, :], (rows_here, block_size)),
            kv_width,
        )
    new_all = lax.all_gather(new_kv, EXP_AXES, axis=0, tiled=True)
    gate_up_local, down_local, new_all = lax.optimization_barrier((w_gate_up[0], w_down[0], new_all))
    gate_up_full, down_full = (
        lax.all_gather(lax.all_gather(gate_up_local, "zlo", axis=0), "req", axis=2, tiled=True),
        lax.all_gather(lax.all_gather(down_local, "zlo", axis=0), "req", axis=3, tiled=True),
    )
    for offset in range(0, new_all.shape[0], key_block):
        block_size = min(key_block, new_all.shape[0] - offset)
        new_pos = offset + jnp.arange(block_size, dtype=jnp.int32)
        running = attend_block(
            running,
            queries,
            new_all[offset : offset + block_size],
            new_pos[None, :] <= query_pos[:, None],
            kv_width,
        )
    run_max, run_sum, run_acc = running
    context = (
        (run_acc / run_sum[..., None])
        .transpose(2, 0, 1, 3)
        .reshape(rows_here, head_count * HEAD_DIM)
        .astype(jnp.bfloat16)
    )
    projected = jnp.dot(context, w_out, preferred_element_type=jnp.float32)
    attended = (hidden_in.astype(jnp.float32) + residual_scale * projected).astype(jnp.bfloat16)
    moe_in = rms_scale(attended, moe_gain)
    block_experts = gate_up_full.shape[1]
    slice_width = down_full.shape[2]
    flat_ids = expert_ids.reshape(-1)
    matches = (flat_ids[:, None] == jnp.arange(EXPERTS, dtype=jnp.int32)[None, :]).astype(jnp.int32)
    pair_count = flat_ids.shape[0]
    earlier = (
        jnp.arange(pair_count, dtype=jnp.int32)[None, :] < jnp.arange(pair_count, dtype=jnp.int32)[:, None]
    ).astype(jnp.bfloat16)
    before = jnp.dot(earlier, matches.astype(jnp.bfloat16), preferred_element_type=jnp.float32)
    slot_rank = jnp.sum(before.astype(jnp.int32) * matches, axis=1)
    slot_index = flat_ids * MOST + slot_rank
    token_of = jnp.arange(flat_ids.shape[0], dtype=jnp.int32) // TOPK
    slot_token = jnp.zeros((EXPERTS * MOST,), jnp.int32).at[slot_index].set(token_of)
    blocks = EXPERTS // block_experts
    outgoing = moe_in[slot_token.reshape(blocks, block_experts, MOST)]
    arrived = lax.all_to_all(outgoing, ("x", "zhi"), split_axis=0, concat_axis=0, tiled=True)
    arrived = lax.all_gather(arrived, "core", axis=0)
    gate_up = jnp.einsum(
        "askmd,pkdf->aspkmf", arrived, gate_up_full, preferred_element_type=jnp.float32
    )
    activated = (jax.nn.silu(gate_up[..., :slice_width]) * gate_up[..., slice_width:]).astype(
        jnp.bfloat16
    )
    computed = jnp.einsum(
        "aspkmf,pkfd->aspkmd", activated, down_full, preferred_element_type=jnp.float32
    ).astype(jnp.bfloat16)
    computed = jnp.sum(computed, axis=2, dtype=jnp.float32)
    mine = lax.dynamic_index_in_dim(computed, core, axis=0, keepdims=False)
    theirs = lax.dynamic_index_in_dim(computed, 1 - core, axis=0, keepdims=False)
    theirs = lax.ppermute(theirs, "core", [(0, 1), (1, 0)])
    computed = (mine + theirs).astype(jnp.bfloat16)
    returned = lax.all_to_all(computed, ("x", "zhi"), split_axis=0, concat_axis=0, tiled=True)
    summed = returned.astype(jnp.float32).reshape(EXPERTS * MOST, width)
    picked = summed[slot_index] * expert_weights.reshape(-1).astype(jnp.float32)[:, None]
    mixture = jnp.sum(picked.reshape(rows_here, TOPK, width), axis=1)
    layer_out = (attended.astype(jnp.float32) + residual_scale * mixture).astype(jnp.bfloat16)
    return (attended, layer_out)


def solution(mesh):
    req_size, exp_size = mesh.shape["req"], mesh.shape["exp"]
    mesh = Mesh(mesh.devices.reshape(req_size, exp_size // 8, 2, 2, 2), ("req",) + EXP_AXES)
    rows = ("req",) + EXP_AXES
    cols = EXP_AXES
    in_specs = (
        P(rows, None),
        P(),
        P(),
        P(),
        P(),
        P(),
        P("req", cols, None),
        P("req"),
        P(),
        P(rows, None),
        P(rows, None),
        P(cols, None, "req", None),
        P(cols, None, None, "req"),
    )
    out_specs = (P(rows, None), P(rows, None))
    return jax.shard_map(shards, mesh=mesh, in_specs=in_specs, out_specs=out_specs, check_vma=False)
```

```python
import jax
import jax.numpy as jnp
from jax import lax
from jax.sharding import Mesh, PartitionSpec as P


HEAD_DIM = 64
EXPERTS = 40
TOPK = 8
MOST = 26


rope_base = 10000.0
attn_scale = 0.015625
residual_scale = 1.0
norm_eps = 1e-06
neg_fill = -1e30
key_block = 512
EXP_AXES = ("x", "zhi", "zlo", "core")


def rms_scale(values, gain):
    widened = values.astype(jnp.float32)
    mean_sq = jnp.mean(widened * widened, axis=-1, keepdims=True)
    return (widened * lax.rsqrt(mean_sq + norm_eps) * gain.astype(jnp.float32)).astype(jnp.bfloat16)


def rotate(projected, positions, head_count, head_dim):
    row_count = projected.shape[0]
    shaped = projected.reshape(row_count, head_count, head_dim)
    half_dim = head_dim // 2
    inverse_freq = rope_base ** (-(jnp.arange(half_dim, dtype=jnp.float32) * 2.0 / head_dim))
    angles = positions.astype(jnp.float32)[:, None] * inverse_freq[None, :]
    cosine = jnp.cos(angles)[:, None, :]
    sinus = jnp.sin(angles)[:, None, :]
    lower_half = shaped[..., :half_dim]
    upper_half = shaped[..., half_dim:]
    turned = jnp.concatenate(
        [lower_half * cosine - upper_half * sinus, upper_half * cosine + lower_half * sinus],
        axis=-1,
    )
    return turned.reshape(row_count, head_count * head_dim).astype(jnp.bfloat16)


def attend_block(running, queries, block_rows, visible, kv_width):
    run_max, run_sum, run_acc = running
    kv_heads = run_max.shape[0]
    head_dim = run_acc.shape[-1]
    block_size = block_rows.shape[0]
    key_heads = block_rows[:, :kv_width].reshape(block_size, kv_heads, head_dim)
    value_heads = block_rows[:, kv_width:].reshape(block_size, kv_heads, head_dim)
    scores = (
        jnp.einsum("tkgd,rkd->kgtr", queries, key_heads, preferred_element_type=jnp.float32)
        * attn_scale
    )
    scores = jnp.where(visible[None, None], scores, neg_fill)
    new_max = jnp.maximum(run_max, jnp.max(scores, axis=-1))
    weights = jnp.where(visible[None, None], jnp.exp(scores - new_max[..., None]), 0.0)
    factor = jnp.exp(run_max - new_max)
    new_sum = run_sum * factor + jnp.sum(weights, axis=-1)
    new_acc = run_acc * factor[..., None] + jnp.einsum(
        "kgtr,rkd->kgtd",
        weights.astype(jnp.bfloat16),
        value_heads,
        preferred_element_type=jnp.float32,
    )
    return (new_max, new_sum, new_acc)


def spread_pieces(local, width_axis):
    req_count = lax.axis_size("req")
    pair = lax.axis_size("zlo")
    stacked = []
    for dz in range(pair):
        chunks = []
        for dr in range(req_count):
            if dr == 0 and dz == 0:
                chunks.append(local)
                continue
            perm = [
                (a * pair + z, ((a + dr) % req_count) * pair + (z + dz) % pair)
                for a in range(req_count)
                for z in range(pair)
            ]
            chunks.append(lax.ppermute(local, ("req", "zlo"), perm))
        stacked.append(jnp.concatenate(chunks, axis=width_axis))
    return jnp.stack(stacked, axis=0)


def in_chunk_order(rows, chunk_order):
    count = chunk_order.shape[0]
    shaped = rows.reshape(rows.shape[0], count, rows.shape[1] // count)
    return jnp.take(shaped, chunk_order, axis=1).reshape(rows.shape)


def shards(
    hidden_in,
    attn_gain,
    w_query,
    w_key,
    w_value,
    w_out,
    cache_kv,
    cache_len,
    moe_gain,
    expert_ids,
    expert_weights,
    w_gate_up,
    w_down,
):
    rows_here = hidden_in.shape[0]
    width = hidden_in.shape[1]
    kv_width = w_key.shape[1]
    kv_heads = kv_width // HEAD_DIM
    head_count = w_query.shape[1] // HEAD_DIM
    group_size = head_count // kv_heads
    core = lax.axis_index("core")
    position_exp = (
        (lax.axis_index("x") * lax.axis_size("zhi") + lax.axis_index("zhi")) * lax.axis_size("zlo")
        + lax.axis_index("zlo")
    ) * lax.axis_size("core") + core
    length = cache_len[0]
    cache_rows = cache_kv[0]
    cache_all = lax.all_gather(cache_rows, EXP_AXES, axis=0, tiled=True)
    gate_up_full = spread_pieces(w_gate_up[0], 1)
    down_full = spread_pieces(w_down[0], 2)
    req_index = lax.axis_index("req")
    chunk_order = (req_index - jnp.arange(lax.axis_size("req"), dtype=jnp.int32)) % lax.axis_size("req")
    normed = rms_scale(hidden_in, attn_gain)
    query_pos = position_exp * rows_here + jnp.arange(rows_here, dtype=jnp.int32)
    positions = length + query_pos
    query = rotate(
        jnp.dot(normed, w_query, preferred_element_type=jnp.float32),
        positions,
        head_count,
        HEAD_DIM,
    )
    keys_new = rotate(
        jnp.dot(normed, w_key, preferred_element_type=jnp.float32), positions, kv_heads, HEAD_DIM
    )
    values_new = jnp.dot(normed, w_value, preferred_element_type=jnp.float32).astype(jnp.bfloat16)
    new_kv = jnp.concatenate([keys_new, values_new], axis=1)
    queries = query.reshape(rows_here, kv_heads, group_size, HEAD_DIM)
    initial = (
        jnp.full((kv_heads, group_size, rows_here), neg_fill, jnp.float32),
        jnp.zeros((kv_heads, group_size, rows_here), jnp.float32),
        jnp.zeros((kv_heads, group_size, rows_here, HEAD_DIM), jnp.float32),
    )
    running = initial
    for offset in range(0, cache_all.shape[0], key_block):
      block_size = min(key_block, cache_all.shape[0] - offset)
      cache_pos = offset + jnp.arange(block_size, dtype=jnp.int32)
      running = attend_block(
          running,
          queries,
          cache_all[offset : offset + block_size],
          jnp.broadcast_to((cache_pos < length)[None, :], (rows_here, block_size)),
          kv_width,
      )
    new_all = lax.all_gather(new_kv, EXP_AXES, axis=0, tiled=True)
    for offset in range(0, new_all.shape[0], key_block):
        block_size = min(key_block, new_all.shape[0] - offset)
        new_pos = offset + jnp.arange(block_size, dtype=jnp.int32)
        running = attend_block(
            running,
            queries,
            new_all[offset : offset + block_size],
            new_pos[None, :] <= query_pos[:, None],
            kv_width,
        )
    _, run_sum, run_acc = running
    context = (
        (run_acc / run_sum[..., None])
        .transpose(2, 0, 1, 3)
        .reshape(rows_here, head_count * HEAD_DIM)
        .astype(jnp.bfloat16)
    )
    projected = jnp.dot(context, w_out, preferred_element_type=jnp.float32)
    attended = (hidden_in.astype(jnp.float32) + residual_scale * projected).astype(jnp.bfloat16)
    moe_in = rms_scale(attended, moe_gain)
    moe_in = in_chunk_order(moe_in, chunk_order)
    block_experts = gate_up_full.shape[1]
    slice_width = down_full.shape[2]
    flat_ids = expert_ids.reshape(-1)
    matches = (flat_ids[:, None] == jnp.arange(EXPERTS, dtype=jnp.int32)[None, :]).astype(jnp.int32)
    pair_count = flat_ids.shape[0]
    earlier = (
        jnp.arange(pair_count, dtype=jnp.int32)[None, :] < jnp.arange(pair_count, dtype=jnp.int32)[:, None]
    ).astype(jnp.bfloat16)
    before = jnp.dot(earlier, matches.astype(jnp.bfloat16), preferred_element_type=jnp.float32)
    slot_rank = jnp.sum(before.astype(jnp.int32) * matches, axis=1)
    slot_index = flat_ids * MOST + slot_rank
    token_of = jnp.arange(flat_ids.shape[0], dtype=jnp.int32) // TOPK
    slot_token = jnp.zeros((EXPERTS * MOST,), jnp.int32).at[slot_index].set(token_of)
    blocks = EXPERTS // block_experts
    outgoing = moe_in[slot_token.reshape(blocks, block_experts, MOST)]
    arrived = lax.all_to_all(outgoing, ("x", "zhi"), split_axis=0, concat_axis=0, tiled=True)
    arrived = lax.all_gather(arrived, "core", axis=0)
    gate_up = jnp.einsum(
        "askmd,pkdf->aspkmf", arrived, gate_up_full, preferred_element_type=jnp.float32
    )
    activated = (jax.nn.silu(gate_up[..., :slice_width]) * gate_up[..., slice_width:]).astype(
        jnp.bfloat16
    )
    computed = jnp.einsum(
        "aspkmf,pkfd->aspkmd", activated, down_full, preferred_element_type=jnp.float32
    ).astype(jnp.bfloat16)
    computed = jnp.sum(computed, axis=2, dtype=jnp.float32)
    mine = lax.dynamic_index_in_dim(computed, core, axis=0, keepdims=False)
    theirs = lax.dynamic_index_in_dim(computed, 1 - core, axis=0, keepdims=False)
    theirs = lax.ppermute(theirs, "core", [(0, 1), (1, 0)])
    computed = (mine + theirs).astype(jnp.bfloat16)
    returned = lax.all_to_all(computed, ("x", "zhi"), split_axis=0, concat_axis=0, tiled=True)
    summed = returned.astype(jnp.float32).reshape(EXPERTS * MOST, width)
    picked = summed[slot_index] * expert_weights.reshape(-1).astype(jnp.float32)[:, None]
    mixture = in_chunk_order(jnp.sum(picked.reshape(rows_here, TOPK, width), axis=1), chunk_order)
    layer_out = (attended.astype(jnp.float32) + residual_scale * mixture).astype(jnp.bfloat16)
    return (attended, layer_out)


def solution(mesh):
    req_size, exp_size = mesh.shape["req"], mesh.shape["exp"]
    mesh = Mesh(mesh.devices.reshape(req_size, exp_size // 8, 2, 2, 2), ("req",) + EXP_AXES)
    rows = ("req",) + EXP_AXES
    cols = EXP_AXES
    in_specs = (
        P(rows, None),
        P(),
        P(),
        P(),
        P(),
        P(),
        P("req", cols, None),
        P("req"),
        P(),
        P(rows, None),
        P(rows, None),
        P(cols, None, "req", None),
        P(cols, None, None, "req"),
    )
    out_specs = (P(rows, None), P(rows, None))

    return jax.shard_map(shards, mesh=mesh, in_specs=in_specs, out_specs=out_specs, check_vma=False)
```

```python
import jax
import jax.numpy as jnp
from jax import lax
from jax.sharding import Mesh, PartitionSpec as P


HEAD_DIM = 64
EXPERTS = 40
TOPK = 8
MOST = 26


rope_base = 10000.0
attn_scale = 0.015625
residual_scale = 1.0
norm_eps = 1e-06
neg_fill = -1e30
key_block = 512
EXP_AXES = ("x", "zhi", "zlo", "core")


def rms_scale(values, gain):
    widened = values.astype(jnp.float32)
    mean_sq = jnp.mean(widened * widened, axis=-1, keepdims=True)
    return (widened * lax.rsqrt(mean_sq + norm_eps) * gain.astype(jnp.float32)).astype(jnp.bfloat16)


def rotate(projected, positions, head_count, head_dim):
    row_count = projected.shape[0]
    shaped = projected.reshape(row_count, head_count, head_dim)
    half_dim = head_dim // 2
    inverse_freq = rope_base ** (-(jnp.arange(half_dim, dtype=jnp.float32) * 2.0 / head_dim))
    angles = positions.astype(jnp.float32)[:, None] * inverse_freq[None, :]
    cosine = jnp.cos(angles)[:, None, :]
    sinus = jnp.sin(angles)[:, None, :]
    lower_half = shaped[..., :half_dim]
    upper_half = shaped[..., half_dim:]
    turned = jnp.concatenate(
        [lower_half * cosine - upper_half * sinus, upper_half * cosine + lower_half * sinus],
        axis=-1,
    )
    return turned.reshape(row_count, head_count * head_dim).astype(jnp.bfloat16)


def attend_block(running, queries, block_rows, visible, kv_width):
    run_max, run_sum, run_acc = running
    kv_heads = run_max.shape[0]
    head_dim = run_acc.shape[-1]
    block_size = block_rows.shape[0]
    key_heads = block_rows[:, :kv_width].reshape(block_size, kv_heads, head_dim)
    value_heads = block_rows[:, kv_width:].reshape(block_size, kv_heads, head_dim)
    scores = (
        jnp.einsum("tkgd,rkd->kgtr", queries, key_heads, preferred_element_type=jnp.float32)
        * attn_scale
    )
    scores = jnp.where(visible[None, None], scores, neg_fill)
    new_max = jnp.maximum(run_max, jnp.max(scores, axis=-1))
    weights = jnp.where(visible[None, None], jnp.exp(scores - new_max[..., None]), 0.0)
    factor = jnp.exp(run_max - new_max)
    new_sum = run_sum * factor + jnp.sum(weights, axis=-1)
    new_acc = run_acc * factor[..., None] + jnp.einsum(
        "kgtr,rkd->kgtd",
        weights.astype(jnp.bfloat16),
        value_heads,
        preferred_element_type=jnp.float32,
    )
    return (new_max, new_sum, new_acc)


def spread_pieces(local, width_axis):
    req_count = lax.axis_size("req")
    pair = lax.axis_size("zlo")
    stacked = []
    for dz in range(pair):
        chunks = []
        for dr in range(req_count):
            if dr == 0 and dz == 0:
                chunks.append(local)
                continue
            perm = [
                (a * pair + z, ((a + dr) % req_count) * pair + (z + dz) % pair)
                for a in range(req_count)
                for z in range(pair)
            ]
            chunks.append(lax.ppermute(local, ("req", "zlo"), perm))
        stacked.append(jnp.concatenate(chunks, axis=width_axis))
    return jnp.stack(stacked, axis=0)


def in_chunk_order(rows, chunk_order):
    count = chunk_order.shape[0]
    shaped = rows.reshape(rows.shape[0], count, rows.shape[1] // count)
    return jnp.take(shaped, chunk_order, axis=1).reshape(rows.shape)


def shards(
    hidden_in,
    attn_gain,
    w_query,
    w_key,
    w_value,
    w_out,
    cache_kv,
    cache_len,
    moe_gain,
    expert_ids,
    expert_weights,
    w_gate_up,
    w_down,
):
    rows_here = hidden_in.shape[0]
    width = hidden_in.shape[1]
    kv_width = w_key.shape[1]
    kv_heads = kv_width // HEAD_DIM
    head_count = w_query.shape[1] // HEAD_DIM
    group_size = head_count // kv_heads
    core = lax.axis_index("core")
    position_exp = (
        (lax.axis_index("x") * lax.axis_size("zhi") + lax.axis_index("zhi")) * lax.axis_size("zlo")
        + lax.axis_index("zlo")
    ) * lax.axis_size("core") + core
    length = cache_len[0]
    cache_rows = cache_kv[0]
    cache_all = lax.all_gather(cache_rows, EXP_AXES, axis=0, tiled=True)
    req_index = lax.axis_index("req")
    chunk_order = (req_index - jnp.arange(lax.axis_size("req"), dtype=jnp.int32)) % lax.axis_size("req")
    normed = rms_scale(hidden_in, attn_gain)
    query_pos = position_exp * rows_here + jnp.arange(rows_here, dtype=jnp.int32)
    positions = length + query_pos
    query = rotate(
        jnp.dot(normed, w_query, preferred_element_type=jnp.float32),
        positions,
        head_count,
        HEAD_DIM,
    )
    keys_new = rotate(
        jnp.dot(normed, w_key, preferred_element_type=jnp.float32), positions, kv_heads, HEAD_DIM
    )
    values_new = jnp.dot(normed, w_value, preferred_element_type=jnp.float32).astype(jnp.bfloat16)
    new_kv = jnp.concatenate([keys_new, values_new], axis=1)
    queries = query.reshape(rows_here, kv_heads, group_size, HEAD_DIM)
    initial = (
        jnp.full((kv_heads, group_size, rows_here), neg_fill, jnp.float32),
        jnp.zeros((kv_heads, group_size, rows_here), jnp.float32),
        jnp.zeros((kv_heads, group_size, rows_here, HEAD_DIM), jnp.float32),
    )
    running = initial
    for offset in range(0, cache_all.shape[0], key_block):
      block_size = min(key_block, cache_all.shape[0] - offset)
      cache_pos = offset + jnp.arange(block_size, dtype=jnp.int32)
      running = attend_block(
          running,
          queries,
          cache_all[offset : offset + block_size],
          jnp.broadcast_to((cache_pos < length)[None, :], (rows_here, block_size)),
          kv_width,
      )
    new_all = lax.all_gather(new_kv, EXP_AXES, axis=0, tiled=True)
    gate_up_local, down_local, new_all = lax.optimization_barrier((w_gate_up[0], w_down[0], new_all))
    gate_up_full = spread_pieces(gate_up_local, 1)
    down_full = spread_pieces(down_local, 2)
    for offset in range(0, new_all.shape[0], key_block):
        block_size = min(key_block, new_all.shape[0] - offset)
        new_pos = offset + jnp.arange(block_size, dtype=jnp.int32)
        running = attend_block(
            running,
            queries,
            new_all[offset : offset + block_size],
            new_pos[None, :] <= query_pos[:, None],
            kv_width,
        )
    _, run_sum, run_acc = running
    context = (
        (run_acc / run_sum[..., None])
        .transpose(2, 0, 1, 3)
        .reshape(rows_here, head_count * HEAD_DIM)
        .astype(jnp.bfloat16)
    )
    projected = jnp.dot(context, w_out, preferred_element_type=jnp.float32)
    attended = (hidden_in.astype(jnp.float32) + residual_scale * projected).astype(jnp.bfloat16)
    moe_in = rms_scale(attended, moe_gain)
    moe_in = in_chunk_order(moe_in, chunk_order)
    block_experts = gate_up_full.shape[1]
    slice_width = down_full.shape[2]
    flat_ids = expert_ids.reshape(-1)
    matches = (flat_ids[:, None] == jnp.arange(EXPERTS, dtype=jnp.int32)[None, :]).astype(jnp.int32)
    pair_count = flat_ids.shape[0]
    earlier = (
        jnp.arange(pair_count, dtype=jnp.int32)[None, :] < jnp.arange(pair_count, dtype=jnp.int32)[:, None]
    ).astype(jnp.bfloat16)
    before = jnp.dot(earlier, matches.astype(jnp.bfloat16), preferred_element_type=jnp.float32)
    slot_rank = jnp.sum(before.astype(jnp.int32) * matches, axis=1)
    slot_index = flat_ids * MOST + slot_rank
    token_of = jnp.arange(flat_ids.shape[0], dtype=jnp.int32) // TOPK
    slot_token = jnp.zeros((EXPERTS * MOST,), jnp.int32).at[slot_index].set(token_of)
    blocks = EXPERTS // block_experts
    outgoing = moe_in[slot_token.reshape(blocks, block_experts, MOST)]
    arrived = lax.all_to_all(outgoing, ("x", "zhi"), split_axis=0, concat_axis=0, tiled=True)
    swap = [(0, 1), (1, 0)]
    arrived = jnp.stack([arrived, lax.ppermute(arrived, "core", swap)], axis=0)
    gate_up = jnp.einsum(
        "askmd,pkdf->aspkmf", arrived, gate_up_full, preferred_element_type=jnp.float32
    )
    activated = (jax.nn.silu(gate_up[..., :slice_width]) * gate_up[..., slice_width:]).astype(
        jnp.bfloat16
    )
    computed = jnp.einsum(
        "aspkmf,pkfd->aspkmd", activated, down_full, preferred_element_type=jnp.float32
    ).astype(jnp.bfloat16)
    computed = jnp.sum(computed, axis=2, dtype=jnp.float32)
    computed = (computed[0] + lax.ppermute(computed[1], "core", swap)).astype(jnp.bfloat16)
    returned = lax.all_to_all(computed, ("x", "zhi"), split_axis=0, concat_axis=0, tiled=True)
    summed = returned.astype(jnp.float32).reshape(EXPERTS * MOST, width)
    picked = summed[slot_index] * expert_weights.reshape(-1).astype(jnp.float32)[:, None]
    mixture = in_chunk_order(jnp.sum(picked.reshape(rows_here, TOPK, width), axis=1), chunk_order)
    layer_out = (attended.astype(jnp.float32) + residual_scale * mixture).astype(jnp.bfloat16)
    return (attended, layer_out)


def solution(mesh):
    req_size, exp_size = mesh.shape["req"], mesh.shape["exp"]
    mesh = Mesh(mesh.devices.reshape(req_size, exp_size // 8, 2, 2, 2), ("req",) + EXP_AXES)
    rows = ("req",) + EXP_AXES
    cols = EXP_AXES
    in_specs = (
        P(rows, None),
        P(),
        P(),
        P(),
        P(),
        P(),
        P("req", cols, None),
        P("req"),
        P(),
        P(rows, None),
        P(rows, None),
        P(cols, None, "req", None),
        P(cols, None, None, "req"),
    )
    out_specs = (P(rows, None), P(rows, None))

    return jax.shard_map(shards, mesh=mesh, in_specs=in_specs, out_specs=out_specs, check_vma=False)
```

```python
import jax
import jax.numpy as jnp
from jax import lax
from jax.experimental import pallas as pl
from jax.experimental.pallas import tpu as pltpu
from jax.sharding import Mesh, PartitionSpec as P


HEAD_DIM = 64
EXPERTS = 40
TOPK = 8
MOST = 26


rope_base = 10000.0
attn_scale = 0.015625
residual_scale = 1.0
norm_eps = 1e-06
neg_fill = -1e30
EXP_AXES = ("x", "zhi", "zlo", "core")


def rms_scale(values, gain):
    widened = values.astype(jnp.float32)
    mean_sq = jnp.mean(widened * widened, axis=-1, keepdims=True)
    return (widened * lax.rsqrt(mean_sq + norm_eps) * gain.astype(jnp.float32)).astype(jnp.bfloat16)


def rotate(projected, positions, head_count, head_dim):
    row_count = projected.shape[0]
    shaped = projected.reshape(row_count, head_count, head_dim)
    half_dim = head_dim // 2
    inverse_freq = rope_base ** (-(jnp.arange(half_dim, dtype=jnp.float32) * 2.0 / head_dim))
    angles = positions.astype(jnp.float32)[:, None] * inverse_freq[None, :]
    cosine = jnp.cos(angles)[:, None, :]
    sinus = jnp.sin(angles)[:, None, :]
    lower_half = shaped[..., :half_dim]
    upper_half = shaped[..., half_dim:]
    turned = jnp.concatenate(
        [lower_half * cosine - upper_half * sinus, upper_half * cosine + lower_half * sinus],
        axis=-1,
    )
    return turned.reshape(row_count, head_count * head_dim).astype(jnp.bfloat16)


INTERPRET = False


def attend(query, cache_all, new_all, bounds, kv_heads, group_size):
    rows = query.shape[0]
    heads_per_step = 128 // HEAD_DIM
    steps = kv_heads // heads_per_step
    q_width = heads_per_step * group_size * HEAD_DIM
    cache_count = cache_all.shape[0]
    new_count = new_all.shape[0]

    def kernel(bounds_ref, q_ref, kc_ref, vc_ref, kn_ref, vn_ref, o_ref):
        length = bounds_ref[0]
        first = bounds_ref[1]
        seen_cache = lax.broadcasted_iota(jnp.int32, (rows, cache_count), 1) < length
        seen_new = lax.broadcasted_iota(jnp.int32, (rows, new_count), 1) <= (
            lax.broadcasted_iota(jnp.int32, (rows, new_count), 0) + first
        )
        pieces = []
        for hh in range(heads_per_step):
            lanes = slice(hh * HEAD_DIM, (hh + 1) * HEAD_DIM)
            kc = kc_ref[:, lanes]
            vc = vc_ref[:, lanes]
            kn = kn_ref[:, lanes]
            vn = vn_ref[:, lanes]
            for g in range(group_size):
                col = (hh * group_size + g) * HEAD_DIM
                q = q_ref[:, col : col + HEAD_DIM]
                dims = (((1,), (1,)), ((), ()))
                s_c = lax.dot_general(q, kc, dims, preferred_element_type=jnp.float32) * attn_scale
                s_n = lax.dot_general(q, kn, dims, preferred_element_type=jnp.float32) * attn_scale
                s_c = jnp.where(seen_cache, s_c, neg_fill)
                s_n = jnp.where(seen_new, s_n, neg_fill)
                top = jnp.maximum(
                    jnp.max(s_c, axis=1, keepdims=True), jnp.max(s_n, axis=1, keepdims=True)
                )
                p_c = jnp.where(seen_cache, jnp.exp(s_c - top), 0.0)
                p_n = jnp.where(seen_new, jnp.exp(s_n - top), 0.0)
                total = jnp.sum(p_c, axis=1, keepdims=True) + jnp.sum(p_n, axis=1, keepdims=True)
                acc = jnp.dot(p_c.astype(jnp.bfloat16), vc, preferred_element_type=jnp.float32)
                acc = acc + jnp.dot(p_n.astype(jnp.bfloat16), vn, preferred_element_type=jnp.float32)
                pieces.append((acc / total).astype(jnp.bfloat16))
        o_ref[...] = jnp.concatenate(pieces, axis=1)

    value_block = kv_heads * HEAD_DIM // 128
    grid_spec = pltpu.PrefetchScalarGridSpec(
        num_scalar_prefetch=1,
        grid=(steps,),
        in_specs=[
            pl.BlockSpec((rows, q_width), lambda i, b: (0, i)),
            pl.BlockSpec((cache_count, 128), lambda i, b: (0, i)),
            pl.BlockSpec((cache_count, 128), lambda i, b: (0, value_block + i)),
            pl.BlockSpec((new_count, 128), lambda i, b: (0, i)),
            pl.BlockSpec((new_count, 128), lambda i, b: (0, value_block + i)),
        ],
        out_specs=pl.BlockSpec((rows, q_width), lambda i, b: (0, i)),
    )
    return pl.pallas_call(
        kernel,
        grid_spec=grid_spec,
        out_shape=jax.ShapeDtypeStruct((rows, query.shape[1]), jnp.bfloat16),
        compiler_params=pltpu.CompilerParams(dimension_semantics=("arbitrary",)),
        interpret=INTERPRET,
    )(bounds, query, cache_all, cache_all, new_all, new_all)


def spread_pieces(local, width_axis):
    req_count = lax.axis_size("req")
    pair = lax.axis_size("zlo")
    stacked = []
    for dz in range(pair):
        chunks = []
        for dr in range(req_count):
            if dr == 0 and dz == 0:
                chunks.append(local)
                continue
            perm = [
                (a * pair + z, ((a + dr) % req_count) * pair + (z + dz) % pair)
                for a in range(req_count)
                for z in range(pair)
            ]
            chunks.append(lax.ppermute(local, ("req", "zlo"), perm))
        stacked.append(jnp.concatenate(chunks, axis=width_axis))
    return jnp.stack(stacked, axis=0)


def in_chunk_order(rows, chunk_order):
    count = chunk_order.shape[0]
    shaped = rows.reshape(rows.shape[0], count, rows.shape[1] // count)
    return jnp.take(shaped, chunk_order, axis=1).reshape(rows.shape)


def shards(
    hidden_in,
    attn_gain,
    w_query,
    w_key,
    w_value,
    w_out,
    cache_kv,
    cache_len,
    moe_gain,
    expert_ids,
    expert_weights,
    w_gate_up,
    w_down,
):
    rows_here = hidden_in.shape[0]
    width = hidden_in.shape[1]
    kv_width = w_key.shape[1]
    kv_heads = kv_width // HEAD_DIM
    head_count = w_query.shape[1] // HEAD_DIM
    group_size = head_count // kv_heads
    core = lax.axis_index("core")
    position_exp = (
        (lax.axis_index("x") * lax.axis_size("zhi") + lax.axis_index("zhi")) * lax.axis_size("zlo")
        + lax.axis_index("zlo")
    ) * lax.axis_size("core") + core
    length = cache_len[0]
    cache_rows = cache_kv[0]
    cache_all = lax.all_gather(cache_rows, EXP_AXES, axis=0, tiled=True)
    req_index = lax.axis_index("req")
    chunk_order = (req_index - jnp.arange(lax.axis_size("req"), dtype=jnp.int32)) % lax.axis_size("req")
    normed = rms_scale(hidden_in, attn_gain)
    query_pos = position_exp * rows_here + jnp.arange(rows_here, dtype=jnp.int32)
    positions = length + query_pos
    query = rotate(
        jnp.dot(normed, w_query, preferred_element_type=jnp.float32),
        positions,
        head_count,
        HEAD_DIM,
    )
    keys_new = rotate(
        jnp.dot(normed, w_key, preferred_element_type=jnp.float32), positions, kv_heads, HEAD_DIM
    )
    values_new = jnp.dot(normed, w_value, preferred_element_type=jnp.float32).astype(jnp.bfloat16)
    new_kv = jnp.concatenate([keys_new, values_new], axis=1)
    new_all = lax.all_gather(new_kv, EXP_AXES, axis=0, tiled=True)
    gate_up_local, down_local, new_all = lax.optimization_barrier((w_gate_up[0], w_down[0], new_all))
    gate_up_full = spread_pieces(gate_up_local, 1)
    down_full = spread_pieces(down_local, 2)
    bounds = jnp.stack([length, position_exp * rows_here]).astype(jnp.int32)
    context = attend(query, cache_all, new_all, bounds, kv_heads, group_size)
    projected = jnp.dot(context, w_out, preferred_element_type=jnp.float32)
    attended = (hidden_in.astype(jnp.float32) + residual_scale * projected).astype(jnp.bfloat16)
    moe_in = rms_scale(attended, moe_gain)
    moe_in = in_chunk_order(moe_in, chunk_order)
    block_experts = gate_up_full.shape[1]
    slice_width = down_full.shape[2]
    flat_ids = expert_ids.reshape(-1)
    matches = (flat_ids[:, None] == jnp.arange(EXPERTS, dtype=jnp.int32)[None, :]).astype(jnp.int32)
    pair_count = flat_ids.shape[0]
    earlier = (
        jnp.arange(pair_count, dtype=jnp.int32)[None, :] < jnp.arange(pair_count, dtype=jnp.int32)[:, None]
    ).astype(jnp.bfloat16)
    before = jnp.dot(earlier, matches.astype(jnp.bfloat16), preferred_element_type=jnp.float32)
    slot_rank = jnp.sum(before.astype(jnp.int32) * matches, axis=1)
    slot_index = flat_ids * MOST + slot_rank
    token_of = jnp.arange(flat_ids.shape[0], dtype=jnp.int32) // TOPK
    slot_token = jnp.zeros((EXPERTS * MOST,), jnp.int32).at[slot_index].set(token_of)
    blocks = EXPERTS // block_experts
    outgoing = moe_in[slot_token.reshape(blocks, block_experts, MOST)]
    arrived = lax.all_to_all(outgoing, ("x", "zhi"), split_axis=0, concat_axis=0, tiled=True)
    swap = [(0, 1), (1, 0)]
    arrived = jnp.stack([arrived, lax.ppermute(arrived, "core", swap)], axis=0)
    gate_up = jnp.einsum(
        "askmd,pkdf->aspkmf", arrived, gate_up_full, preferred_element_type=jnp.float32
    )
    activated = (jax.nn.silu(gate_up[..., :slice_width]) * gate_up[..., slice_width:]).astype(
        jnp.bfloat16
    )
    computed = jnp.einsum(
        "aspkmf,pkfd->aspkmd", activated, down_full, preferred_element_type=jnp.float32
    ).astype(jnp.bfloat16)
    computed = jnp.sum(computed, axis=2, dtype=jnp.float32)
    computed = (computed[0] + lax.ppermute(computed[1], "core", swap)).astype(jnp.bfloat16)
    returned = lax.all_to_all(computed, ("x", "zhi"), split_axis=0, concat_axis=0, tiled=True)
    summed = returned.astype(jnp.float32).reshape(EXPERTS * MOST, width)
    picked = summed[slot_index] * expert_weights.reshape(-1).astype(jnp.float32)[:, None]
    mixture = in_chunk_order(jnp.sum(picked.reshape(rows_here, TOPK, width), axis=1), chunk_order)
    layer_out = (attended.astype(jnp.float32) + residual_scale * mixture).astype(jnp.bfloat16)
    return (attended, layer_out)


def solution(mesh):
    req_size, exp_size = mesh.shape["req"], mesh.shape["exp"]
    mesh = Mesh(mesh.devices.reshape(req_size, exp_size // 8, 2, 2, 2), ("req",) + EXP_AXES)
    rows = ("req",) + EXP_AXES
    cols = EXP_AXES
    in_specs = (
        P(rows, None),
        P(),
        P(),
        P(),
        P(),
        P(),
        P("req", cols, None),
        P("req"),
        P(),
        P(rows, None),
        P(rows, None),
        P(cols, None, "req", None),
        P(cols, None, None, "req"),
    )
    out_specs = (P(rows, None), P(rows, None))

    return jax.shard_map(shards, mesh=mesh, in_specs=in_specs, out_specs=out_specs, check_vma=False)
```

```python
import jax
import jax.numpy as jnp
from jax import lax
from jax.experimental import pallas as pl
from jax.experimental.pallas import tpu as pltpu
from jax.sharding import Mesh, PartitionSpec as P


HEAD_DIM = 64
EXPERTS = 40
TOPK = 8
MOST = 26


rope_base = 10000.0
attn_scale = 0.015625
residual_scale = 1.0
norm_eps = 1e-06
neg_fill = -1e30
EXP_AXES = ("x", "zhi", "zlo", "core")


def rms_scale(values, gain):
    widened = values.astype(jnp.float32)
    mean_sq = jnp.mean(widened * widened, axis=-1, keepdims=True)
    return (widened * lax.rsqrt(mean_sq + norm_eps) * gain.astype(jnp.float32)).astype(jnp.bfloat16)


def rotate(projected, positions, head_count, head_dim):
    row_count = projected.shape[0]
    shaped = projected.reshape(row_count, head_count, head_dim)
    half_dim = head_dim // 2
    inverse_freq = rope_base ** (-(jnp.arange(half_dim, dtype=jnp.float32) * 2.0 / head_dim))
    angles = positions.astype(jnp.float32)[:, None] * inverse_freq[None, :]
    cosine = jnp.cos(angles)[:, None, :]
    sinus = jnp.sin(angles)[:, None, :]
    lower_half = shaped[..., :half_dim]
    upper_half = shaped[..., half_dim:]
    turned = jnp.concatenate(
        [lower_half * cosine - upper_half * sinus, upper_half * cosine + lower_half * sinus],
        axis=-1,
    )
    return turned.reshape(row_count, head_count * head_dim).astype(jnp.bfloat16)


INTERPRET = False


def attend(query, keys, limit, bounds, kv_heads, group_size):
    rows = query.shape[0]
    heads_per_step = 128 // HEAD_DIM
    steps = kv_heads // heads_per_step
    q_width = heads_per_step * group_size * HEAD_DIM
    key_count = keys.shape[0]

    def kernel(bounds_ref, lim_ref, q_ref, k_ref, v_ref, o_ref):
        first = bounds_ref[0]
        seen = lim_ref[...] <= lax.broadcasted_iota(jnp.int32, (rows, key_count), 0) + first
        pieces = []
        for hh in range(heads_per_step):
            lanes = slice(hh * HEAD_DIM, (hh + 1) * HEAD_DIM)
            k = k_ref[:, lanes]
            v = v_ref[:, lanes]
            for g in range(group_size):
                col = (hh * group_size + g) * HEAD_DIM
                q = q_ref[:, col : col + HEAD_DIM]
                dims = (((1,), (1,)), ((), ()))
                scores = lax.dot_general(q, k, dims, preferred_element_type=jnp.float32) * attn_scale
                scores = jnp.where(seen, scores, neg_fill)
                top = jnp.max(scores, axis=1, keepdims=True)
                probs = jnp.where(seen, jnp.exp(scores - top), 0.0)
                total = jnp.sum(probs, axis=1, keepdims=True)
                acc = jnp.dot(probs.astype(jnp.bfloat16), v, preferred_element_type=jnp.float32)
                pieces.append((acc / total).astype(jnp.bfloat16))
        o_ref[...] = jnp.concatenate(pieces, axis=1)

    value_block = kv_heads * HEAD_DIM // 128
    grid_spec = pltpu.PrefetchScalarGridSpec(
        num_scalar_prefetch=1,
        grid=(steps,),
        in_specs=[
            pl.BlockSpec((1, key_count), lambda i, b: (0, 0)),
            pl.BlockSpec((rows, q_width), lambda i, b: (0, i)),
            pl.BlockSpec((key_count, 128), lambda i, b: (0, i)),
            pl.BlockSpec((key_count, 128), lambda i, b: (0, value_block + i)),
        ],
        out_specs=pl.BlockSpec((rows, q_width), lambda i, b: (0, i)),
    )
    return pl.pallas_call(
        kernel,
        grid_spec=grid_spec,
        out_shape=jax.ShapeDtypeStruct((rows, query.shape[1]), jnp.bfloat16),
        compiler_params=pltpu.CompilerParams(dimension_semantics=("arbitrary",)),
        interpret=INTERPRET,
    )(bounds, limit, query, keys, keys)


def spread_pieces(local, width_axis):
    req_count = lax.axis_size("req")
    pair = lax.axis_size("zlo")
    stacked = []
    for dz in range(pair):
        chunks = []
        for dr in range(req_count):
            if dr == 0 and dz == 0:
                chunks.append(local)
                continue
            perm = [
                (a * pair + z, ((a + dr) % req_count) * pair + (z + dz) % pair)
                for a in range(req_count)
                for z in range(pair)
            ]
            chunks.append(lax.ppermute(local, ("req", "zlo"), perm))
        stacked.append(jnp.concatenate(chunks, axis=width_axis))
    return jnp.stack(stacked, axis=0)


def in_chunk_order(rows, chunk_order):
    count = chunk_order.shape[0]
    shaped = rows.reshape(rows.shape[0], count, rows.shape[1] // count)
    return jnp.take(shaped, chunk_order, axis=1).reshape(rows.shape)


def shards(
    hidden_in,
    attn_gain,
    w_query,
    w_key,
    w_value,
    w_out,
    cache_kv,
    cache_len,
    moe_gain,
    expert_ids,
    expert_weights,
    w_gate_up,
    w_down,
):
    rows_here = hidden_in.shape[0]
    width = hidden_in.shape[1]
    kv_width = w_key.shape[1]
    kv_heads = kv_width // HEAD_DIM
    head_count = w_query.shape[1] // HEAD_DIM
    group_size = head_count // kv_heads
    core = lax.axis_index("core")
    position_exp = (
        (lax.axis_index("x") * lax.axis_size("zhi") + lax.axis_index("zhi")) * lax.axis_size("zlo")
        + lax.axis_index("zlo")
    ) * lax.axis_size("core") + core
    length = cache_len[0]
    cache_rows = cache_kv[0]
    cache_count = cache_rows.shape[0]
    req_index = lax.axis_index("req")
    chunk_order = (req_index - jnp.arange(lax.axis_size("req"), dtype=jnp.int32)) % lax.axis_size("req")
    normed = rms_scale(hidden_in, attn_gain)
    query_pos = position_exp * rows_here + jnp.arange(rows_here, dtype=jnp.int32)
    positions = length + query_pos
    query = rotate(
        jnp.dot(normed, w_query, preferred_element_type=jnp.float32),
        positions,
        head_count,
        HEAD_DIM,
    )
    keys_new = rotate(
        jnp.dot(normed, w_key, preferred_element_type=jnp.float32), positions, kv_heads, HEAD_DIM
    )
    values_new = jnp.dot(normed, w_value, preferred_element_type=jnp.float32).astype(jnp.bfloat16)
    new_kv = jnp.concatenate([keys_new, values_new], axis=1)
    joined = jnp.concatenate([cache_rows, new_kv], axis=0)
    piece = lax.all_gather(joined, EXP_AXES, axis=0, tiled=True)
    gate_up_local, down_local, piece = lax.optimization_barrier((w_gate_up[0], w_down[0], piece))
    gate_up_full = spread_pieces(gate_up_local, 1)
    down_full = spread_pieces(down_local, 2)
    shard_rows = cache_count + rows_here
    key_index = jnp.arange(piece.shape[0], dtype=jnp.int32)
    owner = key_index // shard_rows
    within = key_index - owner * shard_rows
    cache_pos = owner * cache_count + within
    new_pos = owner * rows_here + within - cache_count
    never = jnp.int32(2**30)
    limit = jnp.where(
        within < cache_count, jnp.where(cache_pos < length, jnp.int32(-1), never), new_pos
    )
    bounds = (position_exp * rows_here).astype(jnp.int32).reshape(1)
    context = attend(query, piece, limit.reshape(1, -1), bounds, kv_heads, group_size)
    projected = jnp.dot(context, w_out, preferred_element_type=jnp.float32)
    attended = (hidden_in.astype(jnp.float32) + residual_scale * projected).astype(jnp.bfloat16)
    moe_in = rms_scale(attended, moe_gain)
    moe_in = in_chunk_order(moe_in, chunk_order)
    block_experts = gate_up_full.shape[1]
    slice_width = down_full.shape[2]
    flat_ids = expert_ids.reshape(-1)
    matches = (flat_ids[:, None] == jnp.arange(EXPERTS, dtype=jnp.int32)[None, :]).astype(jnp.int32)
    pair_count = flat_ids.shape[0]
    earlier = (
        jnp.arange(pair_count, dtype=jnp.int32)[None, :] < jnp.arange(pair_count, dtype=jnp.int32)[:, None]
    ).astype(jnp.bfloat16)
    before = jnp.dot(earlier, matches.astype(jnp.bfloat16), preferred_element_type=jnp.float32)
    slot_rank = jnp.sum(before.astype(jnp.int32) * matches, axis=1)
    slot_index = flat_ids * MOST + slot_rank
    token_of = jnp.arange(flat_ids.shape[0], dtype=jnp.int32) // TOPK
    slot_token = jnp.zeros((EXPERTS * MOST,), jnp.int32).at[slot_index].set(token_of)
    blocks = EXPERTS // block_experts
    outgoing = moe_in[slot_token.reshape(blocks, block_experts, MOST)]
    arrived = lax.all_to_all(outgoing, ("x", "zhi"), split_axis=0, concat_axis=0, tiled=True)
    swap = [(0, 1), (1, 0)]
    arrived = jnp.stack([arrived, lax.ppermute(arrived, "core", swap)], axis=0)
    gate_up = jnp.einsum(
        "askmd,pkdf->aspkmf", arrived, gate_up_full, preferred_element_type=jnp.float32
    )
    activated = (jax.nn.silu(gate_up[..., :slice_width]) * gate_up[..., slice_width:]).astype(
        jnp.bfloat16
    )
    computed = jnp.einsum(
        "aspkmf,pkfd->aspkmd", activated, down_full, preferred_element_type=jnp.float32
    ).astype(jnp.bfloat16)
    computed = jnp.sum(computed, axis=2, dtype=jnp.float32)
    computed = (computed[0] + lax.ppermute(computed[1], "core", swap)).astype(jnp.bfloat16)
    returned = lax.all_to_all(computed, ("x", "zhi"), split_axis=0, concat_axis=0, tiled=True)
    summed = returned.astype(jnp.float32).reshape(EXPERTS * MOST, width)
    picked = summed[slot_index] * expert_weights.reshape(-1).astype(jnp.float32)[:, None]
    mixture = in_chunk_order(jnp.sum(picked.reshape(rows_here, TOPK, width), axis=1), chunk_order)
    layer_out = (attended.astype(jnp.float32) + residual_scale * mixture).astype(jnp.bfloat16)
    return (attended, layer_out)


def solution(mesh):
    req_size, exp_size = mesh.shape["req"], mesh.shape["exp"]
    mesh = Mesh(mesh.devices.reshape(req_size, exp_size // 8, 2, 2, 2), ("req",) + EXP_AXES)
    rows = ("req",) + EXP_AXES
    cols = EXP_AXES
    in_specs = (
        P(rows, None),
        P(),
        P(),
        P(),
        P(),
        P(),
        P("req", cols, None),
        P("req"),
        P(),
        P(rows, None),
        P(rows, None),
        P(cols, None, "req", None),
        P(cols, None, None, "req"),
    )
    out_specs = (P(rows, None), P(rows, None))

    return jax.shard_map(shards, mesh=mesh, in_specs=in_specs, out_specs=out_specs, check_vma=False)
```

```python
import jax
import jax.numpy as jnp
from jax import lax
from jax.experimental import pallas as pl
from jax.experimental.pallas import tpu as pltpu
from jax.sharding import Mesh, PartitionSpec as P


HEAD_DIM = 64
EXPERTS = 40
TOPK = 8
MOST = 26


rope_base = 10000.0
attn_scale = 0.015625
residual_scale = 1.0
norm_eps = 1e-06
neg_fill = -1e30
EXP_AXES = ("x", "zhi", "zlo", "core")


def rms_scale(values, gain):
    widened = values.astype(jnp.float32)
    mean_sq = jnp.mean(widened * widened, axis=-1, keepdims=True)
    return (widened * lax.rsqrt(mean_sq + norm_eps) * gain.astype(jnp.float32)).astype(jnp.bfloat16)


def rotate(projected, positions, head_count, head_dim):
    row_count = projected.shape[0]
    shaped = projected.reshape(row_count, head_count, head_dim)
    half_dim = head_dim // 2
    inverse_freq = rope_base ** (-(jnp.arange(half_dim, dtype=jnp.float32) * 2.0 / head_dim))
    angles = positions.astype(jnp.float32)[:, None] * inverse_freq[None, :]
    cosine = jnp.cos(angles)[:, None, :]
    sinus = jnp.sin(angles)[:, None, :]
    lower_half = shaped[..., :half_dim]
    upper_half = shaped[..., half_dim:]
    turned = jnp.concatenate(
        [lower_half * cosine - upper_half * sinus, upper_half * cosine + lower_half * sinus],
        axis=-1,
    )
    return turned.reshape(row_count, head_count * head_dim).astype(jnp.bfloat16)


INTERPRET = False


def attend(query, keys, limit, bounds, kv_heads, group_size):
    rows = query.shape[0]
    heads_per_step = 128 // HEAD_DIM
    steps = kv_heads // heads_per_step
    q_width = heads_per_step * group_size * HEAD_DIM
    key_count = keys.shape[0]

    def kernel(bounds_ref, lim_ref, q_ref, k_ref, v_ref, o_ref):
        first = bounds_ref[0]
        seen = lim_ref[...] <= lax.broadcasted_iota(jnp.int32, (rows, key_count), 0) + first
        pieces = []
        for hh in range(heads_per_step):
            lanes = slice(hh * HEAD_DIM, (hh + 1) * HEAD_DIM)
            k = k_ref[:, lanes]
            v = v_ref[:, lanes]
            for g in range(group_size):
                col = (hh * group_size + g) * HEAD_DIM
                q = q_ref[:, col : col + HEAD_DIM]
                dims = (((1,), (1,)), ((), ()))
                scores = lax.dot_general(q, k, dims, preferred_element_type=jnp.float32) * attn_scale
                scores = jnp.where(seen, scores, neg_fill)
                top = jnp.max(scores, axis=1, keepdims=True)
                probs = jnp.where(seen, jnp.exp(scores - top), 0.0)
                total = jnp.sum(probs, axis=1, keepdims=True)
                acc = jnp.dot(probs.astype(jnp.bfloat16), v, preferred_element_type=jnp.float32)
                pieces.append((acc / total).astype(jnp.bfloat16))
        o_ref[...] = jnp.concatenate(pieces, axis=1)

    value_block = kv_heads * HEAD_DIM // 128
    grid_spec = pltpu.PrefetchScalarGridSpec(
        num_scalar_prefetch=1,
        grid=(steps,),
        in_specs=[
            pl.BlockSpec((1, key_count), lambda i, b: (0, 0)),
            pl.BlockSpec((rows, q_width), lambda i, b: (0, i)),
            pl.BlockSpec((key_count, 128), lambda i, b: (0, i)),
            pl.BlockSpec((key_count, 128), lambda i, b: (0, value_block + i)),
        ],
        out_specs=pl.BlockSpec((rows, q_width), lambda i, b: (0, i)),
    )
    return pl.pallas_call(
        kernel,
        grid_spec=grid_spec,
        out_shape=jax.ShapeDtypeStruct((rows, query.shape[1]), jnp.bfloat16),
        compiler_params=pltpu.CompilerParams(dimension_semantics=("arbitrary",)),
        interpret=INTERPRET,
    )(bounds, limit, query, keys, keys)


def spread_pieces(gate_up_local, down_local):
    req_count = lax.axis_size("req")
    pair = lax.axis_size("zlo")
    split = gate_up_local.size
    flat = jnp.concatenate([gate_up_local.reshape(-1), down_local.reshape(-1)])
    gate_up_rows, down_rows = [], []
    for dz in range(pair):
        gate_up_chunks, down_chunks = [], []
        for dr in range(req_count):
            if dr == 0 and dz == 0:
                got = flat
            else:
                perm = [
                    (a * pair + z, ((a + dr) % req_count) * pair + (z + dz) % pair)
                    for a in range(req_count)
                    for z in range(pair)
                ]
                got = lax.ppermute(flat, ("req", "zlo"), perm)
            gate_up_chunks.append(got[:split].reshape(gate_up_local.shape))
            down_chunks.append(got[split:].reshape(down_local.shape))
        gate_up_rows.append(jnp.concatenate(gate_up_chunks, axis=1))
        down_rows.append(jnp.concatenate(down_chunks, axis=2))
    experts, width, both = gate_up_rows[0].shape
    gate_up_full = jnp.stack(gate_up_rows, axis=2).reshape(experts, width, pair * both)
    down_full = jnp.stack(down_rows, axis=1).reshape(experts, pair * down_local.shape[1], width)
    return gate_up_full, down_full


def in_chunk_order(rows, chunk_order):
    count = chunk_order.shape[0]
    shaped = rows.reshape(rows.shape[0], count, rows.shape[1] // count)
    return jnp.take(shaped, chunk_order, axis=1).reshape(rows.shape)


def shards(
    hidden_in,
    attn_gain,
    w_query,
    w_key,
    w_value,
    w_out,
    cache_kv,
    cache_len,
    moe_gain,
    expert_ids,
    expert_weights,
    w_gate_up,
    w_down,
):
    rows_here = hidden_in.shape[0]
    width = hidden_in.shape[1]
    kv_width = w_key.shape[1]
    kv_heads = kv_width // HEAD_DIM
    head_count = w_query.shape[1] // HEAD_DIM
    group_size = head_count // kv_heads
    core = lax.axis_index("core")
    position_exp = (
        (lax.axis_index("x") * lax.axis_size("zhi") + lax.axis_index("zhi")) * lax.axis_size("zlo")
        + lax.axis_index("zlo")
    ) * lax.axis_size("core") + core
    length = cache_len[0]
    cache_rows = cache_kv[0]
    cache_count = cache_rows.shape[0]
    req_index = lax.axis_index("req")
    chunk_order = (req_index - jnp.arange(lax.axis_size("req"), dtype=jnp.int32)) % lax.axis_size("req")
    normed = rms_scale(hidden_in, attn_gain)
    query_pos = position_exp * rows_here + jnp.arange(rows_here, dtype=jnp.int32)
    positions = length + query_pos
    query = rotate(
        jnp.dot(normed, w_query, preferred_element_type=jnp.float32),
        positions,
        head_count,
        HEAD_DIM,
    )
    keys_new = rotate(
        jnp.dot(normed, w_key, preferred_element_type=jnp.float32), positions, kv_heads, HEAD_DIM
    )
    values_new = jnp.dot(normed, w_value, preferred_element_type=jnp.float32).astype(jnp.bfloat16)
    new_kv = jnp.concatenate([keys_new, values_new], axis=1)
    joined = jnp.concatenate([cache_rows, new_kv], axis=0)
    piece = lax.all_gather(joined, EXP_AXES, axis=0, tiled=True)
    gate_up_local, down_local, piece = lax.optimization_barrier((w_gate_up[0], w_down[0], piece))
    gate_up_full, down_full = spread_pieces(gate_up_local, down_local)
    shard_rows = cache_count + rows_here
    key_index = jnp.arange(piece.shape[0], dtype=jnp.int32)
    owner = key_index // shard_rows
    within = key_index - owner * shard_rows
    cache_pos = owner * cache_count + within
    new_pos = owner * rows_here + within - cache_count
    never = jnp.int32(2**30)
    limit = jnp.where(
        within < cache_count, jnp.where(cache_pos < length, jnp.int32(-1), never), new_pos
    )
    bounds = (position_exp * rows_here).astype(jnp.int32).reshape(1)
    context = attend(query, piece, limit.reshape(1, -1), bounds, kv_heads, group_size)
    projected = jnp.dot(context, w_out, preferred_element_type=jnp.float32)
    attended = (hidden_in.astype(jnp.float32) + residual_scale * projected).astype(jnp.bfloat16)
    moe_in = rms_scale(attended, moe_gain)
    moe_in = in_chunk_order(moe_in, chunk_order)
    block_experts = gate_up_full.shape[0]
    slice_width = w_down.shape[2]
    flat_ids = expert_ids.reshape(-1)
    matches = (flat_ids[:, None] == jnp.arange(EXPERTS, dtype=jnp.int32)[None, :]).astype(jnp.int32)
    pair_count = flat_ids.shape[0]
    earlier = (
        jnp.arange(pair_count, dtype=jnp.int32)[None, :] < jnp.arange(pair_count, dtype=jnp.int32)[:, None]
    ).astype(jnp.bfloat16)
    before = jnp.dot(earlier, matches.astype(jnp.bfloat16), preferred_element_type=jnp.float32)
    slot_rank = jnp.sum(before.astype(jnp.int32) * matches, axis=1)
    slot_index = flat_ids * MOST + slot_rank
    token_of = jnp.arange(flat_ids.shape[0], dtype=jnp.int32) // TOPK
    slot_token = jnp.zeros((EXPERTS * MOST,), jnp.int32).at[slot_index].set(token_of)
    blocks = EXPERTS // block_experts
    outgoing = moe_in[slot_token.reshape(blocks, block_experts, MOST)]
    arrived = lax.all_to_all(outgoing, ("x", "zhi"), split_axis=0, concat_axis=0, tiled=True)
    swap = [(0, 1), (1, 0)]

    def experts_on(rows_in):
        gate_up = jnp.einsum("skmd,kdf->skmf", rows_in, gate_up_full, preferred_element_type=jnp.float32)
        gate_up = gate_up.reshape(gate_up.shape[:-1] + (-1, 2 * slice_width))
        activated = (jax.nn.silu(gate_up[..., :slice_width]) * gate_up[..., slice_width:]).astype(
            jnp.bfloat16
        )
        activated = activated.reshape(activated.shape[:-2] + (-1,))
        return jnp.einsum("skmf,kfd->skmd", activated, down_full, preferred_element_type=jnp.float32)

    theirs = experts_on(lax.ppermute(arrived, "core", swap)).astype(jnp.bfloat16)
    theirs = lax.ppermute(theirs, "core", swap)
    computed = (experts_on(arrived) + theirs.astype(jnp.float32)).astype(jnp.bfloat16)
    returned = lax.all_to_all(computed, ("x", "zhi"), split_axis=0, concat_axis=0, tiled=True)
    summed = returned.astype(jnp.float32).reshape(EXPERTS * MOST, width)
    picked = summed[slot_index] * expert_weights.reshape(-1).astype(jnp.float32)[:, None]
    mixture = in_chunk_order(jnp.sum(picked.reshape(rows_here, TOPK, width), axis=1), chunk_order)
    layer_out = (attended.astype(jnp.float32) + residual_scale * mixture).astype(jnp.bfloat16)
    return (attended, layer_out)


def solution(mesh):
    req_size, exp_size = mesh.shape["req"], mesh.shape["exp"]
    mesh = Mesh(mesh.devices.reshape(req_size, exp_size // 8, 2, 2, 2), ("req",) + EXP_AXES)
    rows = ("req",) + EXP_AXES
    cols = EXP_AXES
    in_specs = (
        P(rows, None),
        P(),
        P(),
        P(),
        P(),
        P(),
        P("req", cols, None),
        P("req"),
        P(),
        P(rows, None),
        P(rows, None),
        P(cols, None, "req", None),
        P(cols, None, None, "req"),
    )
    out_specs = (P(rows, None), P(rows, None))

    return jax.shard_map(shards, mesh=mesh, in_specs=in_specs, out_specs=out_specs, check_vma=False)
```

```python
import jax
import jax.numpy as jnp
from jax import lax
from jax.experimental import pallas as pl
from jax.experimental.pallas import tpu as pltpu
from jax.sharding import Mesh, PartitionSpec as P


HEAD_DIM = 64
EXPERTS = 40
TOPK = 8
MOST = 26


rope_base = 10000.0
attn_scale = 0.015625
residual_scale = 1.0
norm_eps = 1e-06
neg_fill = -1e30
EXP_AXES = ("x", "zhi", "zlo", "core")


def rms_scale(values, gain):
    widened = values.astype(jnp.float32)
    mean_sq = jnp.mean(widened * widened, axis=-1, keepdims=True)
    return (widened * lax.rsqrt(mean_sq + norm_eps) * gain.astype(jnp.float32)).astype(jnp.bfloat16)


def rotate(projected, positions, head_count, head_dim):
    row_count = projected.shape[0]
    shaped = projected.reshape(row_count, head_count, head_dim)
    half_dim = head_dim // 2
    inverse_freq = rope_base ** (-(jnp.arange(half_dim, dtype=jnp.float32) * 2.0 / head_dim))
    angles = positions.astype(jnp.float32)[:, None] * inverse_freq[None, :]
    cosine = jnp.cos(angles)[:, None, :]
    sinus = jnp.sin(angles)[:, None, :]
    lower_half = shaped[..., :half_dim]
    upper_half = shaped[..., half_dim:]
    turned = jnp.concatenate(
        [lower_half * cosine - upper_half * sinus, upper_half * cosine + lower_half * sinus],
        axis=-1,
    )
    return turned.reshape(row_count, head_count * head_dim).astype(jnp.bfloat16)


INTERPRET = False


def attend(query, keys, limit, bounds, kv_heads, group_size):
    rows = query.shape[0]
    heads_per_step = 128 // HEAD_DIM
    steps = kv_heads // heads_per_step
    q_width = heads_per_step * group_size * HEAD_DIM
    key_count = keys.shape[0]

    def kernel(bounds_ref, lim_ref, q_ref, k_ref, v_ref, o_ref):
        first = bounds_ref[0]
        seen = lim_ref[...] <= lax.broadcasted_iota(jnp.int32, (rows, key_count), 0) + first
        pieces = []
        for hh in range(heads_per_step):
            lanes = slice(hh * HEAD_DIM, (hh + 1) * HEAD_DIM)
            k = k_ref[:, lanes]
            v = v_ref[:, lanes]
            for g in range(group_size):
                col = (hh * group_size + g) * HEAD_DIM
                q = q_ref[:, col : col + HEAD_DIM]
                dims = (((1,), (1,)), ((), ()))
                scores = lax.dot_general(q, k, dims, preferred_element_type=jnp.float32) * attn_scale
                scores = jnp.where(seen, scores, neg_fill)
                top = jnp.max(scores, axis=1, keepdims=True)
                probs = jnp.where(seen, jnp.exp(scores - top), 0.0)
                total = jnp.sum(probs, axis=1, keepdims=True)
                acc = jnp.dot(probs.astype(jnp.bfloat16), v, preferred_element_type=jnp.float32)
                pieces.append((acc / total).astype(jnp.bfloat16))
        o_ref[...] = jnp.concatenate(pieces, axis=1)

    value_block = kv_heads * HEAD_DIM // 128
    grid_spec = pltpu.PrefetchScalarGridSpec(
        num_scalar_prefetch=1,
        grid=(steps,),
        in_specs=[
            pl.BlockSpec((1, key_count), lambda i, b: (0, 0)),
            pl.BlockSpec((rows, q_width), lambda i, b: (0, i)),
            pl.BlockSpec((key_count, 128), lambda i, b: (0, i)),
            pl.BlockSpec((key_count, 128), lambda i, b: (0, value_block + i)),
        ],
        out_specs=pl.BlockSpec((rows, q_width), lambda i, b: (0, i)),
    )
    return pl.pallas_call(
        kernel,
        grid_spec=grid_spec,
        out_shape=jax.ShapeDtypeStruct((rows, query.shape[1]), jnp.bfloat16),
        compiler_params=pltpu.CompilerParams(dimension_semantics=("arbitrary",)),
        interpret=INTERPRET,
    )(bounds, limit, query, keys, keys)


def spread_pieces(local, width_axis):
    req_count = lax.axis_size("req")
    pair = lax.axis_size("zlo")
    stacked = []
    for dz in range(pair):
        chunks = []
        for dr in range(req_count):
            if dr == 0 and dz == 0:
                chunks.append(local)
                continue
            perm = [
                (a * pair + z, ((a + dr) % req_count) * pair + (z + dz) % pair)
                for a in range(req_count)
                for z in range(pair)
            ]
            chunks.append(lax.ppermute(local, ("req", "zlo"), perm))
        stacked.append(jnp.concatenate(chunks, axis=width_axis))
    return jnp.stack(stacked, axis=0)


def in_chunk_order(rows, chunk_order):
    count = chunk_order.shape[0]
    shaped = rows.reshape(rows.shape[0], count, rows.shape[1] // count)
    return jnp.take(shaped, chunk_order, axis=1).reshape(rows.shape)


def shards(
    hidden_in,
    attn_gain,
    w_query,
    w_key,
    w_value,
    w_out,
    cache_kv,
    cache_len,
    moe_gain,
    expert_ids,
    expert_weights,
    w_gate_up,
    w_down,
):
    rows_here = hidden_in.shape[0]
    width = hidden_in.shape[1]
    kv_width = w_key.shape[1]
    kv_heads = kv_width // HEAD_DIM
    head_count = w_query.shape[1] // HEAD_DIM
    group_size = head_count // kv_heads
    core = lax.axis_index("core")
    position_exp = (
        (lax.axis_index("x") * lax.axis_size("zhi") + lax.axis_index("zhi")) * lax.axis_size("zlo")
        + lax.axis_index("zlo")
    ) * lax.axis_size("core") + core
    length = cache_len[0]
    cache_rows = cache_kv[0]
    cache_count = cache_rows.shape[0]
    req_index = lax.axis_index("req")
    chunk_order = (req_index - jnp.arange(lax.axis_size("req"), dtype=jnp.int32)) % lax.axis_size("req")
    normed = rms_scale(hidden_in, attn_gain)
    query_pos = position_exp * rows_here + jnp.arange(rows_here, dtype=jnp.int32)
    positions = length + query_pos
    query = rotate(
        jnp.dot(normed, w_query, preferred_element_type=jnp.float32),
        positions,
        head_count,
        HEAD_DIM,
    )
    keys_new = rotate(
        jnp.dot(normed, w_key, preferred_element_type=jnp.float32), positions, kv_heads, HEAD_DIM
    )
    values_new = jnp.dot(normed, w_value, preferred_element_type=jnp.float32).astype(jnp.bfloat16)
    new_kv = jnp.concatenate([keys_new, values_new], axis=1)
    joined = jnp.concatenate([cache_rows, new_kv], axis=0)
    piece = lax.all_gather(joined, EXP_AXES, axis=0, tiled=True)
    gate_up_local, down_local, piece = lax.optimization_barrier((w_gate_up[0], w_down[0], piece))
    gate_up_full = spread_pieces(gate_up_local, 1)
    down_full = spread_pieces(down_local, 2)
    shard_rows = cache_count + rows_here
    key_index = jnp.arange(piece.shape[0], dtype=jnp.int32)
    owner = key_index // shard_rows
    within = key_index - owner * shard_rows
    cache_pos = owner * cache_count + within
    new_pos = owner * rows_here + within - cache_count
    never = jnp.int32(2**30)
    limit = jnp.where(
        within < cache_count, jnp.where(cache_pos < length, jnp.int32(-1), never), new_pos
    )
    bounds = (position_exp * rows_here).astype(jnp.int32).reshape(1)
    context = attend(query, piece, limit.reshape(1, -1), bounds, kv_heads, group_size)
    projected = jnp.dot(context, w_out, preferred_element_type=jnp.float32)
    attended = (hidden_in.astype(jnp.float32) + residual_scale * projected).astype(jnp.bfloat16)
    moe_in = rms_scale(attended, moe_gain)
    moe_in = in_chunk_order(moe_in, chunk_order)
    block_experts = gate_up_full.shape[1]
    slice_width = down_full.shape[2]
    flat_ids = expert_ids.reshape(-1)
    matches = (flat_ids[:, None] == jnp.arange(EXPERTS, dtype=jnp.int32)[None, :]).astype(jnp.int32)
    pair_count = flat_ids.shape[0]
    earlier = (
        jnp.arange(pair_count, dtype=jnp.int32)[None, :] < jnp.arange(pair_count, dtype=jnp.int32)[:, None]
    ).astype(jnp.bfloat16)
    before = jnp.dot(earlier, matches.astype(jnp.bfloat16), preferred_element_type=jnp.float32)
    slot_rank = jnp.sum(before.astype(jnp.int32) * matches, axis=1)
    slot_index = flat_ids * MOST + slot_rank
    token_of = jnp.arange(flat_ids.shape[0], dtype=jnp.int32) // TOPK
    slot_token = jnp.zeros((EXPERTS * MOST,), jnp.int32).at[slot_index].set(token_of)
    blocks = EXPERTS // block_experts
    outgoing = moe_in[slot_token.reshape(blocks, block_experts, MOST)]
    arrived = lax.all_to_all(outgoing, ("x", "zhi"), split_axis=0, concat_axis=0, tiled=True)
    swap = [(0, 1), (1, 0)]

    def experts_on(rows_in):
        gate_up = jnp.einsum("skmd,pkdf->spkmf", rows_in, gate_up_full, preferred_element_type=jnp.float32)
        activated = (jax.nn.silu(gate_up[..., :slice_width]) * gate_up[..., slice_width:]).astype(
            jnp.bfloat16
        )
        return jnp.einsum("spkmf,pkfd->skmd", activated, down_full, preferred_element_type=jnp.float32)

    theirs = experts_on(lax.ppermute(arrived, "core", swap)).astype(jnp.bfloat16)
    theirs = lax.ppermute(theirs, "core", swap)
    computed = (experts_on(arrived) + theirs.astype(jnp.float32)).astype(jnp.bfloat16)
    returned = lax.all_to_all(computed, ("x", "zhi"), split_axis=0, concat_axis=0, tiled=True)
    summed = returned.astype(jnp.float32).reshape(EXPERTS * MOST, width)
    picked = summed[slot_index] * expert_weights.reshape(-1).astype(jnp.float32)[:, None]
    mixture = in_chunk_order(jnp.sum(picked.reshape(rows_here, TOPK, width), axis=1), chunk_order)
    layer_out = (attended.astype(jnp.float32) + residual_scale * mixture).astype(jnp.bfloat16)
    return (attended, layer_out)


def solution(mesh):
    req_size, exp_size = mesh.shape["req"], mesh.shape["exp"]
    mesh = Mesh(mesh.devices.reshape(req_size, exp_size // 8, 2, 2, 2), ("req",) + EXP_AXES)
    rows = ("req",) + EXP_AXES
    cols = EXP_AXES
    in_specs = (
        P(rows, None),
        P(),
        P(),
        P(),
        P(),
        P(),
        P("req", cols, None),
        P("req"),
        P(),
        P(rows, None),
        P(rows, None),
        P(cols, None, "req", None),
        P(cols, None, None, "req"),
    )
    out_specs = (P(rows, None), P(rows, None))

    return jax.shard_map(shards, mesh=mesh, in_specs=in_specs, out_specs=out_specs, check_vma=False)
```

```python
import jax
import jax.numpy as jnp
from jax import lax
from jax.experimental import pallas as pl
from jax.experimental.pallas import tpu as pltpu
from jax.sharding import Mesh, PartitionSpec as P


HEAD_DIM = 64
EXPERTS = 40
TOPK = 8
MOST = 26


rope_base = 10000.0
attn_scale = 0.015625
residual_scale = 1.0
norm_eps = 1e-06
neg_fill = -1e30
EXP_AXES = ("x", "zhi", "zlo", "core")


def rms_scale(values, gain):
    widened = values.astype(jnp.float32)
    mean_sq = jnp.mean(widened * widened, axis=-1, keepdims=True)
    return (widened * lax.rsqrt(mean_sq + norm_eps) * gain.astype(jnp.float32)).astype(jnp.bfloat16)


def rotate(projected, positions, head_count, head_dim):
    row_count = projected.shape[0]
    shaped = projected.reshape(row_count, head_count, head_dim)
    half_dim = head_dim // 2
    inverse_freq = rope_base ** (-(jnp.arange(half_dim, dtype=jnp.float32) * 2.0 / head_dim))
    angles = positions.astype(jnp.float32)[:, None] * inverse_freq[None, :]
    cosine = jnp.cos(angles)[:, None, :]
    sinus = jnp.sin(angles)[:, None, :]
    lower_half = shaped[..., :half_dim]
    upper_half = shaped[..., half_dim:]
    turned = jnp.concatenate(
        [lower_half * cosine - upper_half * sinus, upper_half * cosine + lower_half * sinus],
        axis=-1,
    )
    return turned.reshape(row_count, head_count * head_dim).astype(jnp.bfloat16)


INTERPRET = False


def attend(query, keys, limit, bounds, kv_heads, group_size):
    rows = query.shape[0]
    heads_per_step = 128 // HEAD_DIM
    steps = kv_heads // heads_per_step
    q_width = heads_per_step * group_size * HEAD_DIM
    key_count = keys.shape[0]

    def kernel(bounds_ref, lim_ref, q_ref, k_ref, v_ref, o_ref):
        first = bounds_ref[0]
        seen = lim_ref[...] <= lax.broadcasted_iota(jnp.int32, (rows, key_count), 0) + first
        pieces = []
        for hh in range(heads_per_step):
            lanes = slice(hh * HEAD_DIM, (hh + 1) * HEAD_DIM)
            k = k_ref[:, lanes]
            v = v_ref[:, lanes]
            for g in range(group_size):
                col = (hh * group_size + g) * HEAD_DIM
                q = q_ref[:, col : col + HEAD_DIM]
                dims = (((1,), (1,)), ((), ()))
                scores = lax.dot_general(q, k, dims, preferred_element_type=jnp.float32) * attn_scale
                scores = jnp.where(seen, scores, neg_fill)
                top = jnp.max(scores, axis=1, keepdims=True)
                probs = jnp.where(seen, jnp.exp(scores - top), 0.0)
                total = jnp.sum(probs, axis=1, keepdims=True)
                acc = jnp.dot(probs.astype(jnp.bfloat16), v, preferred_element_type=jnp.float32)
                pieces.append((acc / total).astype(jnp.bfloat16))
        o_ref[...] = jnp.concatenate(pieces, axis=1)

    value_block = kv_heads * HEAD_DIM // 128
    grid_spec = pltpu.PrefetchScalarGridSpec(
        num_scalar_prefetch=1,
        grid=(steps,),
        in_specs=[
            pl.BlockSpec((1, key_count), lambda i, b: (0, 0)),
            pl.BlockSpec((rows, q_width), lambda i, b: (0, i)),
            pl.BlockSpec((key_count, 128), lambda i, b: (0, i)),
            pl.BlockSpec((key_count, 128), lambda i, b: (0, value_block + i)),
        ],
        out_specs=pl.BlockSpec((rows, q_width), lambda i, b: (0, i)),
    )
    return pl.pallas_call(
        kernel,
        grid_spec=grid_spec,
        out_shape=jax.ShapeDtypeStruct((rows, query.shape[1]), jnp.bfloat16),
        compiler_params=pltpu.CompilerParams(dimension_semantics=("arbitrary",)),
        interpret=INTERPRET,
    )(bounds, limit, query, keys, keys)


def permute_piece(local, dr, dz):
    req_count = lax.axis_size("req")
    pair = lax.axis_size("zlo")
    perm = [
        (a * pair + z, ((a + dr) % req_count) * pair + (z + dz) % pair)
        for a in range(req_count)
        for z in range(pair)
    ]
    return lax.ppermute(local, ("req", "zlo"), perm)


def spread_pieces(local, width_axis, near, far):
    return jnp.stack(
        [jnp.concatenate([local] + near, axis=width_axis), jnp.concatenate(far, axis=width_axis)],
        axis=0,
    )


def in_chunk_order(rows, chunk_order):
    count = chunk_order.shape[0]
    shaped = rows.reshape(rows.shape[0], count, rows.shape[1] // count)
    return jnp.take(shaped, chunk_order, axis=1).reshape(rows.shape)


def shards(
    hidden_in,
    attn_gain,
    w_query,
    w_key,
    w_value,
    w_out,
    cache_kv,
    cache_len,
    moe_gain,
    expert_ids,
    expert_weights,
    w_gate_up,
    w_down,
):
    rows_here = hidden_in.shape[0]
    width = hidden_in.shape[1]
    kv_width = w_key.shape[1]
    kv_heads = kv_width // HEAD_DIM
    head_count = w_query.shape[1] // HEAD_DIM
    group_size = head_count // kv_heads
    core = lax.axis_index("core")
    position_exp = (
        (lax.axis_index("x") * lax.axis_size("zhi") + lax.axis_index("zhi")) * lax.axis_size("zlo")
        + lax.axis_index("zlo")
    ) * lax.axis_size("core") + core
    length = cache_len[0]
    cache_rows = cache_kv[0]
    cache_count = cache_rows.shape[0]
    req_index = lax.axis_index("req")
    chunk_order = (req_index - jnp.arange(lax.axis_size("req"), dtype=jnp.int32)) % lax.axis_size("req")
    gate_up_near = [permute_piece(w_gate_up[0], dr, 0) for dr in range(1, lax.axis_size("req"))]
    down_near = [permute_piece(w_down[0], dr, 0) for dr in range(1, lax.axis_size("req"))]
    normed = rms_scale(hidden_in, attn_gain)
    query_pos = position_exp * rows_here + jnp.arange(rows_here, dtype=jnp.int32)
    positions = length + query_pos
    query = rotate(
        jnp.dot(normed, w_query, preferred_element_type=jnp.float32),
        positions,
        head_count,
        HEAD_DIM,
    )
    keys_new = rotate(
        jnp.dot(normed, w_key, preferred_element_type=jnp.float32), positions, kv_heads, HEAD_DIM
    )
    values_new = jnp.dot(normed, w_value, preferred_element_type=jnp.float32).astype(jnp.bfloat16)
    new_kv = jnp.concatenate([keys_new, values_new], axis=1)
    joined = jnp.concatenate([cache_rows, new_kv], axis=0)
    piece = lax.all_gather(joined, EXP_AXES, axis=0, tiled=True)
    gate_up_local, down_local, piece = lax.optimization_barrier((w_gate_up[0], w_down[0], piece))
    req_count = lax.axis_size("req")
    gate_up_far = [permute_piece(gate_up_local, dr, 1) for dr in range(req_count)]
    down_far = [permute_piece(down_local, dr, 1) for dr in range(req_count)]
    gate_up_full = spread_pieces(w_gate_up[0], 1, gate_up_near, gate_up_far)
    down_full = spread_pieces(w_down[0], 2, down_near, down_far)
    shard_rows = cache_count + rows_here
    key_index = jnp.arange(piece.shape[0], dtype=jnp.int32)
    owner = key_index // shard_rows
    within = key_index - owner * shard_rows
    cache_pos = owner * cache_count + within
    new_pos = owner * rows_here + within - cache_count
    never = jnp.int32(2**30)
    limit = jnp.where(
        within < cache_count, jnp.where(cache_pos < length, jnp.int32(-1), never), new_pos
    )
    bounds = (position_exp * rows_here).astype(jnp.int32).reshape(1)
    context = attend(query, piece, limit.reshape(1, -1), bounds, kv_heads, group_size)
    projected = jnp.dot(context, w_out, preferred_element_type=jnp.float32)
    attended = (hidden_in.astype(jnp.float32) + residual_scale * projected).astype(jnp.bfloat16)
    moe_in = rms_scale(attended, moe_gain)
    moe_in = in_chunk_order(moe_in, chunk_order)
    block_experts = gate_up_full.shape[1]
    slice_width = down_full.shape[2]
    flat_ids = expert_ids.reshape(-1)
    matches = (flat_ids[:, None] == jnp.arange(EXPERTS, dtype=jnp.int32)[None, :]).astype(jnp.int32)
    pair_count = flat_ids.shape[0]
    earlier = (
        jnp.arange(pair_count, dtype=jnp.int32)[None, :] < jnp.arange(pair_count, dtype=jnp.int32)[:, None]
    ).astype(jnp.bfloat16)
    before = jnp.dot(earlier, matches.astype(jnp.bfloat16), preferred_element_type=jnp.float32)
    slot_rank = jnp.sum(before.astype(jnp.int32) * matches, axis=1)
    slot_index = flat_ids * MOST + slot_rank
    token_of = jnp.arange(flat_ids.shape[0], dtype=jnp.int32) // TOPK
    slot_token = jnp.zeros((EXPERTS * MOST,), jnp.int32).at[slot_index].set(token_of)
    blocks = EXPERTS // block_experts
    outgoing = moe_in[slot_token.reshape(blocks, block_experts, MOST)]
    arrived = lax.all_to_all(outgoing, ("x", "zhi"), split_axis=0, concat_axis=0, tiled=True)
    swap = [(0, 1), (1, 0)]

    def experts_on(rows_in):
        gate_up = jnp.einsum("skmd,pkdf->spkmf", rows_in, gate_up_full, preferred_element_type=jnp.float32)
        activated = (jax.nn.silu(gate_up[..., :slice_width]) * gate_up[..., slice_width:]).astype(
            jnp.bfloat16
        )
        return jnp.einsum("spkmf,pkfd->skmd", activated, down_full, preferred_element_type=jnp.float32)

    theirs = experts_on(lax.ppermute(arrived, "core", swap)).astype(jnp.bfloat16)
    theirs = lax.ppermute(theirs, "core", swap)
    computed = (experts_on(arrived) + theirs.astype(jnp.float32)).astype(jnp.bfloat16)
    returned = lax.all_to_all(computed, ("x", "zhi"), split_axis=0, concat_axis=0, tiled=True)
    summed = returned.astype(jnp.float32).reshape(EXPERTS * MOST, width)
    picked = summed[slot_index] * expert_weights.reshape(-1).astype(jnp.float32)[:, None]
    mixture = in_chunk_order(jnp.sum(picked.reshape(rows_here, TOPK, width), axis=1), chunk_order)
    layer_out = (attended.astype(jnp.float32) + residual_scale * mixture).astype(jnp.bfloat16)
    return (attended, layer_out)


def solution(mesh):
    req_size, exp_size = mesh.shape["req"], mesh.shape["exp"]
    mesh = Mesh(mesh.devices.reshape(req_size, exp_size // 8, 2, 2, 2), ("req",) + EXP_AXES)
    rows = ("req",) + EXP_AXES
    cols = EXP_AXES
    in_specs = (
        P(rows, None),
        P(),
        P(),
        P(),
        P(),
        P(),
        P("req", cols, None),
        P("req"),
        P(),
        P(rows, None),
        P(rows, None),
        P(cols, None, "req", None),
        P(cols, None, None, "req"),
    )
    out_specs = (P(rows, None), P(rows, None))

    return jax.shard_map(shards, mesh=mesh, in_specs=in_specs, out_specs=out_specs, check_vma=False)
```

```python
import jax
import jax.numpy as jnp
from jax import lax
from jax.experimental import pallas as pl
from jax.experimental.pallas import tpu as pltpu
from jax.sharding import Mesh, PartitionSpec as P


HEAD_DIM = 64
EXPERTS = 40
TOPK = 8
MOST = 26


rope_base = 10000.0
attn_scale = 0.015625
residual_scale = 1.0
norm_eps = 1e-06
neg_fill = -1e30
EXP_AXES = ("x", "zhi", "zlo", "core")


def rms_scale(values, gain):
    widened = values.astype(jnp.float32)
    mean_sq = jnp.mean(widened * widened, axis=-1, keepdims=True)
    return (widened * lax.rsqrt(mean_sq + norm_eps) * gain.astype(jnp.float32)).astype(jnp.bfloat16)


def rotate(projected, positions, head_count, head_dim):
    row_count = projected.shape[0]
    shaped = projected.reshape(row_count, head_count, head_dim)
    half_dim = head_dim // 2
    inverse_freq = rope_base ** (-(jnp.arange(half_dim, dtype=jnp.float32) * 2.0 / head_dim))
    angles = positions.astype(jnp.float32)[:, None] * inverse_freq[None, :]
    cosine = jnp.cos(angles)[:, None, :]
    sinus = jnp.sin(angles)[:, None, :]
    lower_half = shaped[..., :half_dim]
    upper_half = shaped[..., half_dim:]
    turned = jnp.concatenate(
        [lower_half * cosine - upper_half * sinus, upper_half * cosine + lower_half * sinus],
        axis=-1,
    )
    return turned.reshape(row_count, head_count * head_dim).astype(jnp.bfloat16)


INTERPRET = False


def attend(query, keys, limit, bounds, kv_heads, group_size):
    rows = query.shape[0]
    heads_per_step = 128 // HEAD_DIM
    steps = kv_heads // heads_per_step
    q_width = heads_per_step * group_size * HEAD_DIM
    key_count = keys.shape[0]

    def kernel(bounds_ref, lim_ref, q_ref, k_ref, v_ref, o_ref):
        first = bounds_ref[0]
        seen = lim_ref[...] <= lax.broadcasted_iota(jnp.int32, (rows, key_count), 0) + first
        pieces = []
        for hh in range(heads_per_step):
            lanes = slice(hh * HEAD_DIM, (hh + 1) * HEAD_DIM)
            k = k_ref[:, lanes]
            v = v_ref[:, lanes]
            for g in range(group_size):
                col = (hh * group_size + g) * HEAD_DIM
                q = q_ref[:, col : col + HEAD_DIM]
                dims = (((1,), (1,)), ((), ()))
                scores = lax.dot_general(q, k, dims, preferred_element_type=jnp.float32) * attn_scale
                scores = jnp.where(seen, scores, neg_fill)
                top = jnp.max(scores, axis=1, keepdims=True)
                probs = jnp.where(seen, jnp.exp(scores - top), 0.0)
                total = jnp.sum(probs, axis=1, keepdims=True)
                acc = jnp.dot(probs.astype(jnp.bfloat16), v, preferred_element_type=jnp.float32)
                pieces.append((acc / total).astype(jnp.bfloat16))
        o_ref[...] = jnp.concatenate(pieces, axis=1)

    value_block = kv_heads * HEAD_DIM // 128
    grid_spec = pltpu.PrefetchScalarGridSpec(
        num_scalar_prefetch=1,
        grid=(steps,),
        in_specs=[
            pl.BlockSpec((1, key_count), lambda i, b: (0, 0)),
            pl.BlockSpec((rows, q_width), lambda i, b: (0, i)),
            pl.BlockSpec((key_count, 128), lambda i, b: (0, i)),
            pl.BlockSpec((key_count, 128), lambda i, b: (0, value_block + i)),
        ],
        out_specs=pl.BlockSpec((rows, q_width), lambda i, b: (0, i)),
    )
    return pl.pallas_call(
        kernel,
        grid_spec=grid_spec,
        out_shape=jax.ShapeDtypeStruct((rows, query.shape[1]), jnp.bfloat16),
        compiler_params=pltpu.CompilerParams(dimension_semantics=("arbitrary",)),
        interpret=INTERPRET,
    )(bounds, limit, query, keys, keys)


def permute_piece(local, dr, dz):
    req_count = lax.axis_size("req")
    pair = lax.axis_size("zlo")
    perm = [
        (a * pair + z, ((a + dr) % req_count) * pair + (z + dz) % pair)
        for a in range(req_count)
        for z in range(pair)
    ]
    return lax.ppermute(local, ("req", "zlo"), perm)


def spread_pieces(local, width_axis, near, far):
    return jnp.stack(
        [jnp.concatenate([local] + near, axis=width_axis), jnp.concatenate(far, axis=width_axis)],
        axis=0,
    )


def in_chunk_order(rows, chunk_order):
    count = chunk_order.shape[0]
    shaped = rows.reshape(rows.shape[0], count, rows.shape[1] // count)
    return jnp.take(shaped, chunk_order, axis=1).reshape(rows.shape)


def shards(
    hidden_in,
    attn_gain,
    w_query,
    w_key,
    w_value,
    w_out,
    cache_kv,
    cache_len,
    moe_gain,
    expert_ids,
    expert_weights,
    w_gate_up,
    w_down,
):
    rows_here = hidden_in.shape[0]
    width = hidden_in.shape[1]
    kv_width = w_key.shape[1]
    kv_heads = kv_width // HEAD_DIM
    head_count = w_query.shape[1] // HEAD_DIM
    group_size = head_count // kv_heads
    core = lax.axis_index("core")
    position_exp = (
        (lax.axis_index("x") * lax.axis_size("zhi") + lax.axis_index("zhi")) * lax.axis_size("zlo")
        + lax.axis_index("zlo")
    ) * lax.axis_size("core") + core
    length = cache_len[0]
    cache_rows = cache_kv[0]
    cache_count = cache_rows.shape[0]
    req_index = lax.axis_index("req")
    chunk_order = (req_index - jnp.arange(lax.axis_size("req"), dtype=jnp.int32)) % lax.axis_size("req")
    gate_up_near = [permute_piece(w_gate_up[0], dr, 0) for dr in range(1, lax.axis_size("req"))]
    down_near = [permute_piece(w_down[0], dr, 0) for dr in range(1, lax.axis_size("req"))]
    normed = rms_scale(hidden_in, attn_gain)
    query_pos = position_exp * rows_here + jnp.arange(rows_here, dtype=jnp.int32)
    positions = length + query_pos
    query = rotate(
        jnp.dot(normed, w_query, preferred_element_type=jnp.float32),
        positions,
        head_count,
        HEAD_DIM,
    )
    keys_new = rotate(
        jnp.dot(normed, w_key, preferred_element_type=jnp.float32), positions, kv_heads, HEAD_DIM
    )
    values_new = jnp.dot(normed, w_value, preferred_element_type=jnp.float32).astype(jnp.bfloat16)
    new_kv = jnp.concatenate([keys_new, values_new], axis=1)
    joined = jnp.concatenate([cache_rows, new_kv], axis=0)
    piece = lax.all_gather(joined, EXP_AXES, axis=0, tiled=True)
    gate_up_local, down_local, piece = lax.optimization_barrier((w_gate_up[0], w_down[0], piece))
    req_count = lax.axis_size("req")
    gate_up_far = [permute_piece(gate_up_local, dr, 1) for dr in range(req_count)]
    down_far = [permute_piece(down_local, dr, 1) for dr in range(req_count)]
    gate_up_full = spread_pieces(w_gate_up[0], 1, gate_up_near, gate_up_far)
    down_full = spread_pieces(w_down[0], 2, down_near, down_far)
    shard_rows = cache_count + rows_here
    key_index = jnp.arange(piece.shape[0], dtype=jnp.int32)
    owner = key_index // shard_rows
    within = key_index - owner * shard_rows
    cache_pos = owner * cache_count + within
    new_pos = owner * rows_here + within - cache_count
    never = jnp.int32(2**30)
    limit = jnp.where(
        within < cache_count, jnp.where(cache_pos < length, jnp.int32(-1), never), new_pos
    )
    bounds = (position_exp * rows_here).astype(jnp.int32).reshape(1)
    context = attend(query, piece, limit.reshape(1, -1), bounds, kv_heads, group_size)
    projected = jnp.dot(context, w_out, preferred_element_type=jnp.float32)
    attended = (hidden_in.astype(jnp.float32) + residual_scale * projected).astype(jnp.bfloat16)
    moe_in = rms_scale(attended, moe_gain)
    moe_in = in_chunk_order(moe_in, chunk_order)
    block_experts = gate_up_full.shape[1]
    slice_width = down_full.shape[2]
    flat_ids = expert_ids.reshape(-1)
    matches = (flat_ids[:, None] == jnp.arange(EXPERTS, dtype=jnp.int32)[None, :]).astype(jnp.int32)
    pair_count = flat_ids.shape[0]
    earlier = (
        jnp.arange(pair_count, dtype=jnp.int32)[None, :] < jnp.arange(pair_count, dtype=jnp.int32)[:, None]
    ).astype(jnp.bfloat16)
    before = jnp.dot(earlier, matches.astype(jnp.bfloat16), preferred_element_type=jnp.float32)
    slot_rank = jnp.sum(before.astype(jnp.int32) * matches, axis=1)
    slot_index = flat_ids * MOST + slot_rank
    token_of = jnp.arange(flat_ids.shape[0], dtype=jnp.int32) // TOPK
    slot_token = jnp.zeros((EXPERTS * MOST,), jnp.int32).at[slot_index].set(token_of)
    blocks = EXPERTS // block_experts
    pick = (slot_token[:, None] == jnp.arange(rows_here, dtype=jnp.int32)[None, :]).astype(jnp.bfloat16)
    outgoing = jnp.dot(pick, moe_in, preferred_element_type=jnp.float32).astype(jnp.bfloat16)
    outgoing = outgoing.reshape(blocks, block_experts, MOST, width)
    arrived = lax.all_to_all(outgoing, ("x", "zhi"), split_axis=0, concat_axis=0, tiled=True)
    swap = [(0, 1), (1, 0)]

    def experts_on(rows_in):
        gate_up = jnp.einsum("skmd,pkdf->spkmf", rows_in, gate_up_full, preferred_element_type=jnp.float32)
        activated = (jax.nn.silu(gate_up[..., :slice_width]) * gate_up[..., slice_width:]).astype(
            jnp.bfloat16
        )
        return jnp.einsum("spkmf,pkfd->skmd", activated, down_full, preferred_element_type=jnp.float32)

    theirs = experts_on(lax.ppermute(arrived, "core", swap)).astype(jnp.bfloat16)
    theirs = lax.ppermute(theirs, "core", swap)
    computed = (experts_on(arrived) + theirs.astype(jnp.float32)).astype(jnp.bfloat16)
    returned = lax.all_to_all(computed, ("x", "zhi"), split_axis=0, concat_axis=0, tiled=True)
    mixing = (
        jnp.zeros((rows_here, EXPERTS * MOST), jnp.bfloat16)
        .at[token_of, slot_index]
        .set(expert_weights.reshape(-1))
    )
    mixture = jnp.dot(
        mixing, returned.reshape(EXPERTS * MOST, width), preferred_element_type=jnp.float32
    )
    mixture = in_chunk_order(mixture, chunk_order)
    layer_out = (attended.astype(jnp.float32) + residual_scale * mixture).astype(jnp.bfloat16)
    return (attended, layer_out)


def solution(mesh):
    req_size, exp_size = mesh.shape["req"], mesh.shape["exp"]
    mesh = Mesh(mesh.devices.reshape(req_size, exp_size // 8, 2, 2, 2), ("req",) + EXP_AXES)
    rows = ("req",) + EXP_AXES
    cols = EXP_AXES
    in_specs = (
        P(rows, None),
        P(),
        P(),
        P(),
        P(),
        P(),
        P("req", cols, None),
        P("req"),
        P(),
        P(rows, None),
        P(rows, None),
        P(cols, None, "req", None),
        P(cols, None, None, "req"),
    )
    out_specs = (P(rows, None), P(rows, None))

    return jax.shard_map(shards, mesh=mesh, in_specs=in_specs, out_specs=out_specs, check_vma=False)
```
